256 devices in a mesh: neuron: 16 (over z, x_hi), tm: 16 (over y, x_lo, core).
Axes of the slice: x: 4 (x_hi: 2, x_lo: 2; x = x_hi * 2 + x_lo), y: 4, z: 8, core: 2. Of those that a mesh axis runs over, the one named last changes fastest.
Arguments:
- signal: bfloat16 [8192, 65536], P('tm', 'neuron'), may hold values from -6 to 6
- readin: bfloat16 [65536, 256], P('neuron'), may hold values from -0.0234375 to 0.0234375
- proj: bfloat16 [256, 512], replicated, may hold values from -0.375 to 0.375
- kernel: float32 [63, 512], replicated, may hold values from -0.75 to 0.75
- gain: float32 [512], replicated, may hold values from 0.5 to 1.5
- w_one: bfloat16 [512, 2048], P(None, 'neuron'), may hold values from -0.25 to 0.25
- w_two: bfloat16 [2048, 512], P('neuron'), may hold values from -0.125 to 0.125
- cotangent: bfloat16 [8192, 512], P('tm'), may hold values from -6 to 6
Outputs:
- denoised: bfloat16 [8192, 512], P('tm')
- grad_readin: float32 [65536, 256], P(('neuron', 'tm'))
- grad_proj: float32 [256, 512], replicated
- grad_kernel: float32 [63, 512], replicated
- grad_gain: float32 [512], replicated
- grad_w_one: float32 [512, 2048], P(None, 'neuron')
- grad_w_two: float32 [2048, 512], P('neuron')
The draws below stay inside these ranges and needn't reach their ends.
All inputs are finite; a program needn't handle non-finite values.
Results may differ from the reference program's by a relative error of at most 0.0085.
Values may be sent and summed in bfloat16 or wider, within the bound.
No kernel may reach another device: no remote copies, remote signals or barrier semaphores. Data moves between devices by JAX's collectives and lax.ppermute only.
A program may use at most 64 MiB of HBM per device.

```python
import jax
import jax.numpy as jnp
from jax import lax

NEURONS = 65536
LAT = 256
DM = 512
HID = 2048
KW = 63
HALF = 31
TIME = 8192


def spiked(values, key, source, target, blocks, factor):
    def block_of(dim):
        return (jnp.arange(values.shape[dim]) // (values.shape[dim] // blocks)).reshape((-1,) + (1,) * (values.ndim - 1 - dim))

    first = jax.random.permutation(key, blocks)[block_of(target)]
    other_side = (block_of(target) + blocks // 2) % blocks
    return jnp.where((block_of(source) == first) | (block_of(source) == other_side), factor * values, values)


def level_of(key, extent, shards, low, largest):
    factor_of = 1.0
    for axis_at, parts in shards:
        draws = jax.random.uniform(jax.random.fold_in(jax.random.fold_in(key, 6), axis_at), (parts,), jnp.float32, low / len(shards), largest / len(shards))
        factor_of = factor_of * jnp.repeat(jnp.exp(draws), extent[axis_at] // parts).reshape((-1,) + (1,) * (len(extent) - 1 - axis_at))
    return factor_of


def gaussian(stream_key, dims, deviation, most, pieces=(), kind=jnp.bfloat16):
    values = jax.random.normal(stream_key, dims, jnp.float32) * deviation
    if len(pieces) > 0:
        values = level_of(stream_key, dims, pieces, -0.22, 0.18) * values
    return jnp.clip(values, min=-most, max=most).astype(kind)


def heavy_noise(stream_key, extent, spread, most, cuts, heavy, held_as=jnp.bfloat16):
    result = spread * jax.random.normal(stream_key, extent, jnp.float32)
    if cuts:
        result = result * level_of(stream_key, extent, cuts, -0.22, 0.18)
    return jnp.clip(spiked(result, jax.random.fold_in(stream_key, 3), *heavy), -most, most).astype(held_as)


def setup_inputs(seed: int = 0) -> dict:
    arg_keys = jax.random.split(jax.random.key(seed), 9)
    return {
        "signal": heavy_noise(arg_keys[0], (TIME, NEURONS), 1.0, 6.0, ((0, 16), (1, 16)), (0, 1, 16, 2.0)),
        "readin": gaussian(arg_keys[1], (NEURONS, LAT), NEURONS ** -0.5, 0.0234375, ((0, 16),)),
        "proj": gaussian(arg_keys[2], (LAT, DM), LAT ** -0.5, 0.375),
        "kernel": gaussian(arg_keys[3], (KW, DM), KW ** -0.5, 0.75, (), jnp.float32),
        "gain": jnp.clip(1.0 + 0.1 * jax.random.normal(arg_keys[4], (DM,), jnp.float32), 0.5, 1.5),
        "w_one": gaussian(arg_keys[5], (DM, HID), DM ** -0.5, 0.25, ((1, 16),)),
        "w_two": gaussian(arg_keys[6], (HID, DM), HID ** -0.5, 0.125, ((0, 16),)),
        "cotangent": gaussian(arg_keys[7], (TIME, DM), 1.0, 6.0, ((0, 16),)),
    }


def conv_time(padded, kernel, rows):

    def step(index, total):
        window = lax.dynamic_slice_in_dim(padded, index, rows, 0).astype(jnp.float32)
        taps = lax.dynamic_slice_in_dim(kernel, index, 1, 0)
        return total + taps * window
    start = jnp.zeros((rows, padded.shape[1]), jnp.float32)
    return lax.fori_loop(0, kernel.shape[0], step, start)

def reference(signal, readin, proj, kernel, gain, w_one, w_two, cotangent):
    latent = jnp.dot(signal, readin, preferred_element_type=jnp.float32).astype(jnp.bfloat16)
    lifted = jnp.dot(latent, proj, preferred_element_type=jnp.float32)
    padded = jnp.pad(lifted, ((HALF, HALF), (0, 0)))
    mixed = lifted + conv_time(padded, kernel, TIME)
    scale = lax.rsqrt(lax.optimization_barrier(jnp.mean(mixed * mixed, axis=1, keepdims=True)) + 1e-05)
    normed = (mixed * scale * gain[None, :]).astype(jnp.bfloat16)
    pre = jnp.dot(normed, w_one, preferred_element_type=jnp.float32)
    act = jax.nn.silu(pre).astype(jnp.bfloat16)
    denoised = (mixed + jnp.dot(act, w_two, preferred_element_type=jnp.float32)).astype(jnp.bfloat16)
    grad_w_two = jnp.dot(act.T, cotangent, preferred_element_type=jnp.float32)
    dact = jnp.dot(cotangent, w_two.T, preferred_element_type=jnp.float32)
    sig = jax.nn.sigmoid(pre)
    dpre = (dact * sig * (1.0 + pre * (1.0 - sig))).astype(jnp.bfloat16)
    grad_w_one = jnp.dot(normed.T, dpre, preferred_element_type=jnp.float32)
    dnormed = jnp.dot(dpre, w_one.T, preferred_element_type=jnp.float32)
    grad_gain = lax.optimization_barrier(jnp.sum(dnormed * mixed * scale, axis=0))
    dgained = dnormed * gain[None, :]
    inner = lax.optimization_barrier(jnp.mean(dgained * mixed, axis=1, keepdims=True))
    dmixed = cotangent.astype(jnp.float32) + scale * dgained - mixed * scale ** 3 * inner

    def kernel_row(index):
        window = lax.dynamic_slice_in_dim(padded, index, TIME, 0).astype(jnp.float32)
        return lax.optimization_barrier(jnp.sum(dmixed * window, axis=0))
    grad_kernel = lax.map(kernel_row, jnp.arange(KW, dtype=jnp.int32))
    padded_grad = jnp.pad(dmixed, ((HALF, HALF), (0, 0)))
    dlifted = (dmixed + conv_time(padded_grad, kernel[::-1], TIME)).astype(jnp.bfloat16)
    grad_proj = jnp.dot(latent.T, dlifted, preferred_element_type=jnp.float32)
    dlatent = jnp.dot(dlifted, proj.T, preferred_element_type=jnp.float32).astype(jnp.bfloat16)
    grad_readin = jnp.dot(signal.T, dlatent, preferred_element_type=jnp.float32)
    return (denoised, grad_readin, grad_proj, grad_kernel, grad_gain, grad_w_one, grad_w_two)
```

```python
import jax
import jax.numpy as jnp
from jax import lax
from jax.experimental import pallas as pl
from jax.sharding import PartitionSpec as P

LANES = 128
CHUNK = 128
RCHUNK = 64


def with_halo(block, sides, width):
    for axis, dim in sides:
        count = lax.axis_size(axis)
        forward = [(i, i + 1) for i in range(count - 1)]
        backward = [(target, source) for source, target in forward]
        low = lax.ppermute(
            lax.slice_in_dim(block, block.shape[dim] - width, None, axis=dim), axis, forward
        )
        high = lax.ppermute(lax.slice_in_dim(block, 0, width, axis=dim), axis, backward)
        block = jnp.concatenate([low, block, high], axis=dim)
    return block


def _fwd_conv_kernel(x_ref, mid_ref, k_ref, o_ref):
    rows, lanes = o_ref.shape
    taps = k_ref.shape[0]
    for r0 in range(0, rows, CHUNK):
        acc = jnp.zeros((CHUNK, lanes), jnp.float32)
        for j in range(taps):
            acc = acc + k_ref[pl.ds(j, 1), :] * x_ref[pl.ds(r0 + j, CHUNK), :]
        o_ref[pl.ds(r0, CHUNK), :] = mid_ref[pl.ds(r0, CHUNK), :] + acc


def fwd_conv(padded, mid, kernel):
    rows, width = mid.shape
    taps = kernel.shape[0]
    return pl.pallas_call(
        _fwd_conv_kernel,
        out_shape=jax.ShapeDtypeStruct((rows, width), jnp.float32),
        grid=(width // LANES,),
        in_specs=[
            pl.BlockSpec((padded.shape[0], LANES), lambda c: (0, c)),
            pl.BlockSpec((rows, LANES), lambda c: (0, c)),
            pl.BlockSpec((taps, LANES), lambda c: (0, c)),
        ],
        out_specs=pl.BlockSpec((rows, LANES), lambda c: (0, c)),
    )(padded, mid, kernel)


def _bwd_conv_kernel(g_ref, d_ref, x_ref, k_ref, dl_ref, gk_ref):
    rows, lanes = dl_ref.shape
    taps = k_ref.shape[0]
    for r0 in range(0, rows, CHUNK):
        acc = jnp.zeros((CHUNK, lanes), jnp.float32)
        for j in range(taps):
            acc = acc + k_ref[pl.ds(taps - 1 - j, 1), :] * g_ref[pl.ds(r0 + j, CHUNK), :]
        dl_ref[pl.ds(r0, CHUNK), :] = (d_ref[pl.ds(r0, CHUNK), :] + acc).astype(dl_ref.dtype)
    for j in range(taps):
        part = jnp.zeros((8, lanes), jnp.float32)
        for r0 in range(0, rows, RCHUNK):
            prod = d_ref[pl.ds(r0, RCHUNK), :] * x_ref[pl.ds(r0 + j, RCHUNK), :]
            part = part + prod.reshape(RCHUNK // 8, 8, lanes).sum(axis=0)
        gk_ref[pl.ds(j, 1), :] = part.sum(axis=0, keepdims=True)


def bwd_conv(padded_grad, dmixed, padded, kernel):
    rows, width = dmixed.shape
    taps = kernel.shape[0]
    full = padded.shape[0]
    return pl.pallas_call(
        _bwd_conv_kernel,
        out_shape=(
            jax.ShapeDtypeStruct((rows, width), jnp.bfloat16),
            jax.ShapeDtypeStruct((taps, width), jnp.float32),
        ),
        grid=(width // LANES,),
        in_specs=[
            pl.BlockSpec((full, LANES), lambda c: (0, c)),
            pl.BlockSpec((rows, LANES), lambda c: (0, c)),
            pl.BlockSpec((full, LANES), lambda c: (0, c)),
            pl.BlockSpec((taps, LANES), lambda c: (0, c)),
        ],
        out_specs=(
            pl.BlockSpec((rows, LANES), lambda c: (0, c)),
            pl.BlockSpec((taps, LANES), lambda c: (0, c)),
        ),
    )(padded_grad, dmixed, padded, kernel)


def over_time(left, right):
    return lax.dot_general(
        left, right, (((0,), (0,)), ((), ())), preferred_element_type=jnp.float32
    )


def body(signal, readin, proj, kernel, gain, w_one, w_two, cotangent):
    taps = kernel.shape[0]
    half = (taps - 1) // 2
    partial_latent = jnp.dot(signal, readin, preferred_element_type=jnp.float32)
    latent = lax.psum(partial_latent, "neuron").astype(jnp.bfloat16)
    lifted = jnp.dot(latent, proj, preferred_element_type=jnp.float32)
    padded = with_halo(lifted, (("tm", 0),), half)
    mixed = fwd_conv(padded, lifted, kernel)
    scale = lax.rsqrt(jnp.mean(mixed * mixed, axis=1, keepdims=True) + 1e-05)
    normed = (mixed * scale * gain[None, :]).astype(jnp.bfloat16)
    pre = jnp.dot(normed, w_one, preferred_element_type=jnp.float32)
    act = jax.nn.silu(pre).astype(jnp.bfloat16)
    partial_mix = jnp.dot(act, w_two, preferred_element_type=jnp.float32)
    denoised = (mixed + lax.psum(partial_mix, "neuron")).astype(jnp.bfloat16)
    local_w_two = over_time(act, cotangent)
    dact = jnp.dot(cotangent, w_two.T, preferred_element_type=jnp.float32)
    sig = jax.nn.sigmoid(pre)
    dpre = (dact * sig * (1.0 + pre * (1.0 - sig))).astype(jnp.bfloat16)
    local_w_one = over_time(normed, dpre)
    partial_normed = jnp.dot(dpre, w_one.T, preferred_element_type=jnp.float32)
    dnormed = lax.psum(partial_normed, "neuron")
    local_gain = jnp.sum(dnormed * mixed * scale, axis=0)
    dgained = dnormed * gain[None, :]
    inner = jnp.mean(dgained * mixed, axis=1, keepdims=True)
    dmixed = cotangent.astype(jnp.float32) + scale * dgained - mixed * scale**3 * inner
    padded_grad = with_halo(dmixed, (("tm", 0),), half)
    dlifted, local_kernel = bwd_conv(padded_grad, dmixed, padded, kernel)
    local_proj = over_time(latent, dlifted)
    dlatent = jnp.dot(dlifted, proj.T, preferred_element_type=jnp.float32).astype(jnp.bfloat16)
    local_small = jnp.concatenate([local_kernel, local_gain[None, :]], axis=0)
    grad_w_one, grad_w_two, grad_small, grad_proj = lax.psum(
        (local_w_one, local_w_two, local_small, local_proj), "tm"
    )
    grad_kernel = grad_small[:taps]
    grad_gain = grad_small[taps]
    grad_readin = lax.psum_scatter(
        over_time(signal, dlatent), "tm", scatter_dimension=0, tiled=True
    )
    return (denoised, grad_readin, grad_proj, grad_kernel, grad_gain, grad_w_one, grad_w_two)


def solution(mesh):
    in_specs = (
        P("tm", "neuron"),
        P("neuron", None),
        P(),
        P(),
        P(),
        P(None, "neuron"),
        P("neuron", None),
        P("tm", None),
    )
    out_specs = (
        P("tm", None),
        P(("neuron", "tm"), None),
        P(),
        P(),
        P(),
        P(None, "neuron"),
        P("neuron", None),
    )
    return jax.shard_map(body, mesh=mesh, in_specs=in_specs, out_specs=out_specs, check_vma=False)
```

```python
import jax
import jax.numpy as jnp
from jax import lax
from jax.experimental import pallas as pl
from jax.sharding import PartitionSpec as P

LANES = 128
CHUNK = 128
RCHUNK = 64


def with_halo(block, sides, width):
    for axis, dim in sides:
        count = lax.axis_size(axis)
        forward = [(i, i + 1) for i in range(count - 1)]
        backward = [(target, source) for source, target in forward]
        low = lax.ppermute(
            lax.slice_in_dim(block, block.shape[dim] - width, None, axis=dim), axis, forward
        )
        high = lax.ppermute(lax.slice_in_dim(block, 0, width, axis=dim), axis, backward)
        block = jnp.concatenate([low, block, high], axis=dim)
    return block


def _fwd_conv_kernel(x_ref, mid_ref, k_ref, o_ref):
    rows, lanes = o_ref.shape
    taps = k_ref.shape[0]
    for r0 in range(0, rows, CHUNK):
        acc = jnp.zeros((CHUNK, lanes), jnp.float32)
        for j in range(taps):
            acc = acc + k_ref[pl.ds(j, 1), :] * x_ref[pl.ds(r0 + j, CHUNK), :]
        o_ref[pl.ds(r0, CHUNK), :] = mid_ref[pl.ds(r0, CHUNK), :] + acc


def fwd_conv(padded, mid, kernel):
    rows, width = mid.shape
    taps = kernel.shape[0]
    return pl.pallas_call(
        _fwd_conv_kernel,
        out_shape=jax.ShapeDtypeStruct((rows, width), jnp.float32),
        grid=(width // LANES,),
        in_specs=[
            pl.BlockSpec((padded.shape[0], LANES), lambda c: (0, c)),
            pl.BlockSpec((rows, LANES), lambda c: (0, c)),
            pl.BlockSpec((taps, LANES), lambda c: (0, c)),
        ],
        out_specs=pl.BlockSpec((rows, LANES), lambda c: (0, c)),
    )(padded, mid, kernel)


def _bwd_conv_kernel(g_ref, d_ref, x_ref, k_ref, dl_ref, gk_ref):
    rows, lanes = dl_ref.shape
    taps = k_ref.shape[0]
    for r0 in range(0, rows, CHUNK):
        acc = jnp.zeros((CHUNK, lanes), jnp.float32)
        for j in range(taps):
            acc = acc + k_ref[pl.ds(taps - 1 - j, 1), :] * g_ref[pl.ds(r0 + j, CHUNK), :]
        dl_ref[pl.ds(r0, CHUNK), :] = (d_ref[pl.ds(r0, CHUNK), :] + acc).astype(dl_ref.dtype)
    for j in range(taps):
        part = jnp.zeros((8, lanes), jnp.float32)
        for r0 in range(0, rows, RCHUNK):
            prod = d_ref[pl.ds(r0, RCHUNK), :] * x_ref[pl.ds(r0 + j, RCHUNK), :]
            part = part + prod.reshape(RCHUNK // 8, 8, lanes).sum(axis=0)
        gk_ref[pl.ds(j, 1), :] = part.sum(axis=0, keepdims=True)


def bwd_conv(padded_grad, dmixed, padded, kernel):
    rows, width = dmixed.shape
    taps = kernel.shape[0]
    full = padded.shape[0]
    return pl.pallas_call(
        _bwd_conv_kernel,
        out_shape=(
            jax.ShapeDtypeStruct((rows, width), jnp.bfloat16),
            jax.ShapeDtypeStruct((taps, width), jnp.float32),
        ),
        grid=(width // LANES,),
        in_specs=[
            pl.BlockSpec((full, LANES), lambda c: (0, c)),
            pl.BlockSpec((rows, LANES), lambda c: (0, c)),
            pl.BlockSpec((full, LANES), lambda c: (0, c)),
            pl.BlockSpec((taps, LANES), lambda c: (0, c)),
        ],
        out_specs=(
            pl.BlockSpec((rows, LANES), lambda c: (0, c)),
            pl.BlockSpec((taps, LANES), lambda c: (0, c)),
        ),
    )(padded_grad, dmixed, padded, kernel)


def over_time(left, right):
    return lax.dot_general(
        left, right, (((0,), (0,)), ((), ())), preferred_element_type=jnp.float32
    )


def scatter_sum(parts, axis):
    got = lax.all_to_all(parts, axis, 0, 0, tiled=False)
    return jnp.sum(got, axis=0)


def gather_all(piece, axis):
    count = lax.axis_size(axis)
    spread = jnp.broadcast_to(piece[None], (count,) + piece.shape)
    return lax.all_to_all(spread, axis, 0, 0, tiled=False)


def split_rows(x, count):
    return x.reshape((count, x.shape[0] // count) + x.shape[1:])


def body(signal, readin, proj, kernel, gain, w_one, w_two, cotangent):
    rows = signal.shape[0]
    taps = kernel.shape[0]
    half = (taps - 1) // 2
    nn = lax.axis_size("neuron")
    nt = lax.axis_size("tm")
    me = lax.axis_index("neuron")
    share = rows // nn
    partial_latent = jnp.dot(signal, readin, preferred_element_type=jnp.float32)
    latent_rows = scatter_sum(split_rows(partial_latent, nn), "neuron").astype(jnp.bfloat16)
    latent = gather_all(latent_rows, "neuron").reshape(rows, -1)
    lifted = jnp.dot(latent, proj, preferred_element_type=jnp.float32)
    padded = with_halo(lifted, (("tm", 0),), half)
    mixed = fwd_conv(padded, lifted, kernel)
    scale = lax.rsqrt(jnp.mean(mixed * mixed, axis=1, keepdims=True) + 1e-05)
    normed = (mixed * scale * gain[None, :]).astype(jnp.bfloat16)
    pre = jnp.dot(normed, w_one, preferred_element_type=jnp.float32)
    act = jax.nn.silu(pre).astype(jnp.bfloat16)
    partial_mix = jnp.dot(act, w_two, preferred_element_type=jnp.float32)
    local_w_two = over_time(act, cotangent)
    dact = jnp.dot(cotangent, w_two.T, preferred_element_type=jnp.float32)
    sig = jax.nn.sigmoid(pre)
    dpre = (dact * sig * (1.0 + pre * (1.0 - sig))).astype(jnp.bfloat16)
    local_w_one = over_time(normed, dpre)
    grad_w_one, grad_w_two = lax.psum((local_w_one, local_w_two), "tm")
    partial_normed = jnp.dot(dpre, w_one.T, preferred_element_type=jnp.float32)
    both = jnp.stack([split_rows(partial_mix, nn), split_rows(partial_normed, nn)], axis=1)
    summed = scatter_sum(both, "neuron")
    mixed_rows = lax.dynamic_slice_in_dim(mixed, me * share, share, 0)
    denoised_rows = (mixed_rows + summed[0]).astype(jnp.bfloat16).astype(jnp.float32)
    back = gather_all(jnp.stack([denoised_rows, summed[1]]), "neuron")
    denoised = back[:, 0].reshape(rows, -1).astype(jnp.bfloat16)
    dnormed = back[:, 1].reshape(rows, -1)
    local_gain = jnp.sum(dnormed * mixed * scale, axis=0)
    dgained = dnormed * gain[None, :]
    inner = jnp.mean(dgained * mixed, axis=1, keepdims=True)
    dmixed = cotangent.astype(jnp.float32) + scale * dgained - mixed * scale**3 * inner
    padded_grad = with_halo(dmixed, (("tm", 0),), half)
    dlifted, local_kernel = bwd_conv(padded_grad, dmixed, padded, kernel)
    local_proj = over_time(latent, dlifted)
    dlatent = jnp.dot(dlifted, proj.T, preferred_element_type=jnp.float32).astype(jnp.bfloat16)
    local_readin = over_time(signal, dlatent)
    small = jnp.concatenate(
        [local_proj.reshape(-1), local_kernel.reshape(-1), local_gain.reshape(-1)]
    )
    readin_part = local_readin.reshape(nt, -1)
    packed = jnp.concatenate([readin_part, small.reshape(nt, -1)], axis=1)
    reduced = scatter_sum(packed, "tm")
    cut = readin_part.shape[1]
    grad_readin = reduced[:cut].reshape(-1, local_readin.shape[1])
    small_sum = gather_all(reduced[cut:], "tm").reshape(-1)
    n_proj = local_proj.size
    n_kernel = local_kernel.size
    grad_proj = small_sum[:n_proj].reshape(local_proj.shape)
    grad_kernel = small_sum[n_proj:n_proj + n_kernel].reshape(local_kernel.shape)
    grad_gain = small_sum[n_proj + n_kernel:]
    return (denoised, grad_readin, grad_proj, grad_kernel, grad_gain, grad_w_one, grad_w_two)


def solution(mesh):
    in_specs = (
        P("tm", "neuron"),
        P("neuron", None),
        P(),
        P(),
        P(),
        P(None, "neuron"),
        P("neuron", None),
        P("tm", None),
    )
    out_specs = (
        P("tm", None),
        P(("neuron", "tm"), None),
        P(),
        P(),
        P(),
        P(None, "neuron"),
        P("neuron", None),
    )
    return jax.shard_map(body, mesh=mesh, in_specs=in_specs, out_specs=out_specs, check_vma=False)
```

```python
import jax
import jax.numpy as jnp
from jax import lax
from jax.experimental import pallas as pl
from jax.sharding import PartitionSpec as P

LANES = 128
CHUNK = 128
RCHUNK = 64


def with_halo(block, sides, width):
    for axis, dim in sides:
        count = lax.axis_size(axis)
        forward = [(i, i + 1) for i in range(count - 1)]
        backward = [(target, source) for source, target in forward]
        low = lax.ppermute(
            lax.slice_in_dim(block, block.shape[dim] - width, None, axis=dim), axis, forward
        )
        high = lax.ppermute(lax.slice_in_dim(block, 0, width, axis=dim), axis, backward)
        block = jnp.concatenate([low, block, high], axis=dim)
    return block


def _fwd_conv_kernel(x_ref, mid_ref, k_ref, o_ref):
    rows, lanes = o_ref.shape
    taps = k_ref.shape[0]
    for r0 in range(0, rows, CHUNK):
        acc = jnp.zeros((CHUNK, lanes), jnp.float32)
        for j in range(taps):
            acc = acc + k_ref[pl.ds(j, 1), :] * x_ref[pl.ds(r0 + j, CHUNK), :]
        o_ref[pl.ds(r0, CHUNK), :] = mid_ref[pl.ds(r0, CHUNK), :] + acc


def fwd_conv(padded, mid, kernel):
    rows, width = mid.shape
    taps = kernel.shape[0]
    return pl.pallas_call(
        _fwd_conv_kernel,
        out_shape=jax.ShapeDtypeStruct((rows, width), jnp.float32),
        grid=(width // LANES,),
        in_specs=[
            pl.BlockSpec((padded.shape[0], LANES), lambda c: (0, c)),
            pl.BlockSpec((rows, LANES), lambda c: (0, c)),
            pl.BlockSpec((taps, LANES), lambda c: (0, c)),
        ],
        out_specs=pl.BlockSpec((rows, LANES), lambda c: (0, c)),
    )(padded, mid, kernel)


def _bwd_conv_kernel(g_ref, d_ref, x_ref, k_ref, dl_ref, gk_ref):
    rows, lanes = dl_ref.shape
    taps = k_ref.shape[0]
    for r0 in range(0, rows, CHUNK):
        acc = jnp.zeros((CHUNK, lanes), jnp.float32)
        for j in range(taps):
            acc = acc + k_ref[pl.ds(taps - 1 - j, 1), :] * g_ref[pl.ds(r0 + j, CHUNK), :]
        dl_ref[pl.ds(r0, CHUNK), :] = (d_ref[pl.ds(r0, CHUNK), :] + acc).astype(dl_ref.dtype)
    for j in range(taps):
        part = jnp.zeros((8, lanes), jnp.float32)
        for r0 in range(0, rows, RCHUNK):
            prod = d_ref[pl.ds(r0, RCHUNK), :] * x_ref[pl.ds(r0 + j, RCHUNK), :]
            part = part + prod.reshape(RCHUNK // 8, 8, lanes).sum(axis=0)
        gk_ref[pl.ds(j, 1), :] = part.sum(axis=0, keepdims=True)


def bwd_conv(padded_grad, dmixed, padded, kernel):
    rows, width = dmixed.shape
    taps = kernel.shape[0]
    full = padded.shape[0]
    return pl.pallas_call(
        _bwd_conv_kernel,
        out_shape=(
            jax.ShapeDtypeStruct((rows, width), jnp.bfloat16),
            jax.ShapeDtypeStruct((taps, width), jnp.float32),
        ),
        grid=(width // LANES,),
        in_specs=[
            pl.BlockSpec((full, LANES), lambda c: (0, c)),
            pl.BlockSpec((rows, LANES), lambda c: (0, c)),
            pl.BlockSpec((full, LANES), lambda c: (0, c)),
            pl.BlockSpec((taps, LANES), lambda c: (0, c)),
        ],
        out_specs=(
            pl.BlockSpec((rows, LANES), lambda c: (0, c)),
            pl.BlockSpec((taps, LANES), lambda c: (0, c)),
        ),
    )(padded_grad, dmixed, padded, kernel)


def over_time(left, right):
    return lax.dot_general(
        left, right, (((0,), (0,)), ((), ())), preferred_element_type=jnp.float32
    )


def scatter_sum(parts, axis):
    got = lax.all_to_all(parts, axis, 0, 0, tiled=False)
    return jnp.sum(got, axis=0)


def gather_all(piece, axis):
    count = lax.axis_size(axis)
    spread = jnp.broadcast_to(piece[None], (count,) + piece.shape)
    return lax.all_to_all(spread, axis, 0, 0, tiled=False)


def split_rows(x, count):
    return x.reshape((count, x.shape[0] // count) + x.shape[1:])


def body(signal, readin, proj, kernel, gain, w_one, w_two, cotangent):
    rows = signal.shape[0]
    taps = kernel.shape[0]
    half = (taps - 1) // 2
    nn = lax.axis_size("neuron")
    nt = lax.axis_size("tm")
    me = lax.axis_index("neuron")
    share = rows // nn
    partial_latent = jnp.dot(signal, readin, preferred_element_type=jnp.float32)
    latent_rows = scatter_sum(split_rows(partial_latent, nn), "neuron").astype(jnp.bfloat16)
    latent = gather_all(latent_rows, "neuron").reshape(rows, -1)
    lifted = jnp.dot(latent, proj, preferred_element_type=jnp.float32)
    padded = with_halo(lifted, (("tm", 0),), half)
    mixed = fwd_conv(padded, lifted, kernel)
    scale = lax.rsqrt(jnp.mean(mixed * mixed, axis=1, keepdims=True) + 1e-05)
    normed = (mixed * scale * gain[None, :]).astype(jnp.bfloat16)
    pre = jnp.dot(normed, w_one, preferred_element_type=jnp.float32)
    act = jax.nn.silu(pre).astype(jnp.bfloat16)
    partial_mix = jnp.dot(act, w_two, preferred_element_type=jnp.float32)
    local_w_two = over_time(act, cotangent)
    dact = jnp.dot(cotangent, w_two.T, preferred_element_type=jnp.float32)
    sig = jax.nn.sigmoid(pre)
    dpre = (dact * sig * (1.0 + pre * (1.0 - sig))).astype(jnp.bfloat16)
    local_w_one = over_time(normed, dpre)
    partial_normed = jnp.dot(dpre, w_one.T, preferred_element_type=jnp.float32)
    both = jnp.stack([split_rows(partial_mix, nn), split_rows(partial_normed, nn)], axis=1)
    summed = scatter_sum(both, "neuron")
    mixed_rows = lax.dynamic_slice_in_dim(mixed, me * share, share, 0)
    denoised_rows = (mixed_rows + summed[0]).astype(jnp.bfloat16).astype(jnp.float32)
    back = gather_all(jnp.stack([denoised_rows, summed[1]]), "neuron")
    denoised = back[:, 0].reshape(rows, -1).astype(jnp.bfloat16)
    dnormed = back[:, 1].reshape(rows, -1)
    local_gain = jnp.sum(dnormed * mixed * scale, axis=0)
    dgained = dnormed * gain[None, :]
    inner = jnp.mean(dgained * mixed, axis=1, keepdims=True)
    dmixed = cotangent.astype(jnp.float32) + scale * dgained - mixed * scale**3 * inner
    padded_grad = with_halo(dmixed, (("tm", 0),), half)
    dlifted, local_kernel = bwd_conv(padded_grad, dmixed, padded, kernel)
    local_proj = over_time(latent, dlifted)
    dlatent = jnp.dot(dlifted, proj.T, preferred_element_type=jnp.float32).astype(jnp.bfloat16)
    local_readin = over_time(signal, dlatent)
    grads = (local_proj, local_kernel, local_gain, local_w_one, local_w_two)
    width = local_readin.shape[1]
    small = jnp.concatenate([g.reshape(-1) for g in grads]).reshape(nt, -1, width)
    readin_part = local_readin.reshape(nt, -1, width)
    cut = readin_part.shape[1]
    reduced = scatter_sum(jnp.concatenate([readin_part, small], axis=1), "tm")
    grad_readin = reduced[:cut]
    small_sum = gather_all(reduced[cut:], "tm").reshape(-1)
    outs = []
    at = 0
    for g in grads:
        outs.append(small_sum[at:at + g.size].reshape(g.shape))
        at += g.size
    grad_proj, grad_kernel, grad_gain, grad_w_one, grad_w_two = outs
    return (denoised, grad_readin, grad_proj, grad_kernel, grad_gain, grad_w_one, grad_w_two)


def solution(mesh):
    in_specs = (
        P("tm", "neuron"),
        P("neuron", None),
        P(),
        P(),
        P(),
        P(None, "neuron"),
        P("neuron", None),
        P("tm", None),
    )
    out_specs = (
        P("tm", None),
        P(("neuron", "tm"), None),
        P(),
        P(),
        P(),
        P(None, "neuron"),
        P("neuron", None),
    )
    return jax.shard_map(body, mesh=mesh, in_specs=in_specs, out_specs=out_specs, check_vma=False)
```

```python
import jax
import jax.numpy as jnp
from jax import lax
from jax.experimental import pallas as pl
from jax.sharding import PartitionSpec as P

LANES = 128
CHUNK = 128
RCHUNK = 64


def with_halo(block, sides, width):
    for axis, dim in sides:
        count = lax.axis_size(axis)
        forward = [(i, i + 1) for i in range(count - 1)]
        backward = [(target, source) for source, target in forward]
        low = lax.ppermute(
            lax.slice_in_dim(block, block.shape[dim] - width, None, axis=dim), axis, forward
        )
        high = lax.ppermute(lax.slice_in_dim(block, 0, width, axis=dim), axis, backward)
        block = jnp.concatenate([low, block, high], axis=dim)
    return block


def _fwd_conv_kernel(x_ref, mid_ref, k_ref, o_ref):
    rows, lanes = o_ref.shape
    taps = k_ref.shape[0]
    for r0 in range(0, rows, CHUNK):
        acc = jnp.zeros((CHUNK, lanes), jnp.float32)
        for j in range(taps):
            acc = acc + k_ref[pl.ds(j, 1), :] * x_ref[pl.ds(r0 + j, CHUNK), :]
        o_ref[pl.ds(r0, CHUNK), :] = mid_ref[pl.ds(r0, CHUNK), :] + acc


def fwd_conv(padded, mid, kernel):
    rows, width = mid.shape
    taps = kernel.shape[0]
    return pl.pallas_call(
        _fwd_conv_kernel,
        out_shape=jax.ShapeDtypeStruct((rows, width), jnp.float32),
        grid=(width // LANES,),
        in_specs=[
            pl.BlockSpec((padded.shape[0], LANES), lambda c: (0, c)),
            pl.BlockSpec((rows, LANES), lambda c: (0, c)),
            pl.BlockSpec((taps, LANES), lambda c: (0, c)),
        ],
        out_specs=pl.BlockSpec((rows, LANES), lambda c: (0, c)),
    )(padded, mid, kernel)


def _bwd_conv_kernel(g_ref, d_ref, x_ref, k_ref, dl_ref, gk_ref):
    rows, lanes = dl_ref.shape
    taps = k_ref.shape[0]
    for r0 in range(0, rows, CHUNK):
        acc = jnp.zeros((CHUNK, lanes), jnp.float32)
        for j in range(taps):
            acc = acc + k_ref[pl.ds(taps - 1 - j, 1), :] * g_ref[pl.ds(r0 + j, CHUNK), :]
        dl_ref[pl.ds(r0, CHUNK), :] = (d_ref[pl.ds(r0, CHUNK), :] + acc).astype(dl_ref.dtype)
    for j in range(taps):
        part = jnp.zeros((8, lanes), jnp.float32)
        for r0 in range(0, rows, RCHUNK):
            prod = d_ref[pl.ds(r0, RCHUNK), :] * x_ref[pl.ds(r0 + j, RCHUNK), :]
            part = part + prod.reshape(RCHUNK // 8, 8, lanes).sum(axis=0)
        gk_ref[pl.ds(j, 1), :] = part.sum(axis=0, keepdims=True)


def bwd_conv(padded_grad, dmixed, padded, kernel):
    rows, width = dmixed.shape
    taps = kernel.shape[0]
    full = padded.shape[0]
    return pl.pallas_call(
        _bwd_conv_kernel,
        out_shape=(
            jax.ShapeDtypeStruct((rows, width), jnp.bfloat16),
            jax.ShapeDtypeStruct((taps, width), jnp.float32),
        ),
        grid=(width // LANES,),
        in_specs=[
            pl.BlockSpec((full, LANES), lambda c: (0, c)),
            pl.BlockSpec((rows, LANES), lambda c: (0, c)),
            pl.BlockSpec((full, LANES), lambda c: (0, c)),
            pl.BlockSpec((taps, LANES), lambda c: (0, c)),
        ],
        out_specs=(
            pl.BlockSpec((rows, LANES), lambda c: (0, c)),
            pl.BlockSpec((taps, LANES), lambda c: (0, c)),
        ),
    )(padded_grad, dmixed, padded, kernel)


def over_time(left, right):
    return lax.dot_general(
        left, right, (((0,), (0,)), ((), ())), preferred_element_type=jnp.float32
    )


def scatter_sum(parts, axis):
    got = lax.all_to_all(parts, axis, 0, 0, tiled=False)
    return jnp.sum(got, axis=0)


def gather_all(piece, axis):
    count = lax.axis_size(axis)
    spread = jnp.broadcast_to(piece[None], (count,) + piece.shape)
    return lax.all_to_all(spread, axis, 0, 0, tiled=False)


def split_rows(x, count):
    return x.reshape((count, x.shape[0] // count) + x.shape[1:])


def body(signal, readin, proj, kernel, gain, w_one, w_two, cotangent):
    rows = signal.shape[0]
    taps = kernel.shape[0]
    half = (taps - 1) // 2
    nn = lax.axis_size("neuron")
    nt = lax.axis_size("tm")
    me = lax.axis_index("neuron")
    share = rows // nn
    partial_latent = jnp.dot(signal, readin, preferred_element_type=jnp.float32)
    latent_rows = scatter_sum(split_rows(partial_latent, nn), "neuron").astype(jnp.bfloat16)
    latent = gather_all(latent_rows, "neuron").reshape(rows, -1)
    lifted = jnp.dot(latent, proj, preferred_element_type=jnp.float32)
    padded = with_halo(lifted, (("tm", 0),), half)
    mixed = fwd_conv(padded, lifted, kernel)
    scale = lax.rsqrt(jnp.mean(mixed * mixed, axis=1, keepdims=True) + 1e-05)
    normed = (mixed * scale * gain[None, :]).astype(jnp.bfloat16)
    pre = jnp.dot(normed, w_one, preferred_element_type=jnp.float32)
    act = jax.nn.silu(pre).astype(jnp.bfloat16)
    partial_mix = jnp.dot(act, w_two, preferred_element_type=jnp.float32)
    local_w_two = over_time(act, cotangent)
    dact = jnp.dot(cotangent, w_two.T, preferred_element_type=jnp.float32)
    sig = jax.nn.sigmoid(pre)
    dpre = (dact * sig * (1.0 + pre * (1.0 - sig))).astype(jnp.bfloat16)
    local_w_one = over_time(normed, dpre)
    partial_normed = jnp.dot(dpre, w_one.T, preferred_element_type=jnp.float32)
    dnormed_rows = scatter_sum(split_rows(partial_normed, nn), "neuron")
    dnormed = gather_all(dnormed_rows, "neuron").reshape(rows, -1)
    mix_rows = scatter_sum(split_rows(partial_mix, nn), "neuron")
    mixed_rows = lax.dynamic_slice_in_dim(mixed, me * share, share, 0)
    denoised_rows = (mixed_rows + mix_rows).astype(jnp.bfloat16)
    denoised = gather_all(denoised_rows, "neuron").reshape(rows, -1)
    local_gain = jnp.sum(dnormed * mixed * scale, axis=0)
    dgained = dnormed * gain[None, :]
    inner = jnp.mean(dgained * mixed, axis=1, keepdims=True)
    dmixed = cotangent.astype(jnp.float32) + scale * dgained - mixed * scale**3 * inner
    padded_grad = with_halo(dmixed, (("tm", 0),), half)
    dlifted, local_kernel = bwd_conv(padded_grad, dmixed, padded, kernel)
    local_proj = over_time(latent, dlifted)
    dlatent = jnp.dot(dlifted, proj.T, preferred_element_type=jnp.float32).astype(jnp.bfloat16)
    local_readin = over_time(signal, dlatent)
    grads = (local_proj, local_kernel, local_gain, local_w_one, local_w_two)
    width = local_readin.shape[1]
    small = jnp.concatenate([g.reshape(-1, width) for g in grads]).reshape(nt, -1, width)
    readin_part = local_readin.reshape(nt, -1, width)
    cut = readin_part.shape[1]
    reduced = scatter_sum(jnp.concatenate([readin_part, small], axis=1), "tm")
    grad_readin = reduced[:cut]
    small_sum = gather_all(reduced[cut:], "tm").reshape(-1, width)
    outs = []
    at = 0
    for g in grads:
        count = g.size // width
        outs.append(small_sum[at:at + count].reshape(g.shape))
        at += count
    grad_proj, grad_kernel, grad_gain, grad_w_one, grad_w_two = outs
    return (denoised, grad_readin, grad_proj, grad_kernel, grad_gain, grad_w_one, grad_w_two)


def solution(mesh):
    in_specs = (
        P("tm", "neuron"),
        P("neuron", None),
        P(),
        P(),
        P(),
        P(None, "neuron"),
        P("neuron", None),
        P("tm", None),
    )
    out_specs = (
        P("tm", None),
        P(("neuron", "tm"), None),
        P(),
        P(),
        P(),
        P(None, "neuron"),
        P("neuron", None),
    )
    return jax.shard_map(body, mesh=mesh, in_specs=in_specs, out_specs=out_specs, check_vma=False)
```

```python
import jax
import jax.numpy as jnp
from jax import lax
from jax.experimental import pallas as pl
from jax.sharding import PartitionSpec as P

LANES = 128
CHUNK = 128
RCHUNK = 64


def with_halo(block, sides, width):
    for axis, dim in sides:
        count = lax.axis_size(axis)
        forward = [(i, i + 1) for i in range(count - 1)]
        backward = [(target, source) for source, target in forward]
        low = lax.ppermute(
            lax.slice_in_dim(block, block.shape[dim] - width, None, axis=dim), axis, forward
        )
        high = lax.ppermute(lax.slice_in_dim(block, 0, width, axis=dim), axis, backward)
        block = jnp.concatenate([low, block, high], axis=dim)
    return block


def _fwd_conv_kernel(x_ref, mid_ref, k_ref, o_ref):
    rows, lanes = o_ref.shape
    taps = k_ref.shape[0]
    for r0 in range(0, rows, CHUNK):
        acc = jnp.zeros((CHUNK, lanes), jnp.float32)
        for j in range(taps):
            acc = acc + k_ref[pl.ds(j, 1), :] * x_ref[pl.ds(r0 + j, CHUNK), :]
        o_ref[pl.ds(r0, CHUNK), :] = mid_ref[pl.ds(r0, CHUNK), :] + acc


def fwd_conv(padded, mid, kernel):
    rows, width = mid.shape
    taps = kernel.shape[0]
    return pl.pallas_call(
        _fwd_conv_kernel,
        out_shape=jax.ShapeDtypeStruct((rows, width), jnp.float32),
        grid=(width // LANES,),
        in_specs=[
            pl.BlockSpec((padded.shape[0], LANES), lambda c: (0, c)),
            pl.BlockSpec((rows, LANES), lambda c: (0, c)),
            pl.BlockSpec((taps, LANES), lambda c: (0, c)),
        ],
        out_specs=pl.BlockSpec((rows, LANES), lambda c: (0, c)),
    )(padded, mid, kernel)


def _bwd_conv_kernel(g_ref, d_ref, x_ref, k_ref, dl_ref, gk_ref):
    rows, lanes = dl_ref.shape
    taps = k_ref.shape[0]
    for r0 in range(0, rows, CHUNK):
        acc = jnp.zeros((CHUNK, lanes), jnp.float32)
        for j in range(taps):
            acc = acc + k_ref[pl.ds(taps - 1 - j, 1), :] * g_ref[pl.ds(r0 + j, CHUNK), :]
        dl_ref[pl.ds(r0, CHUNK), :] = (d_ref[pl.ds(r0, CHUNK), :] + acc).astype(dl_ref.dtype)
    for j in range(taps):
        part = jnp.zeros((8, lanes), jnp.float32)
        for r0 in range(0, rows, RCHUNK):
            prod = d_ref[pl.ds(r0, RCHUNK), :] * x_ref[pl.ds(r0 + j, RCHUNK), :]
            part = part + prod.reshape(RCHUNK // 8, 8, lanes).sum(axis=0)
        gk_ref[pl.ds(j, 1), :] = part.sum(axis=0, keepdims=True)


def bwd_conv(padded_grad, dmixed, padded, kernel):
    rows, width = dmixed.shape
    taps = kernel.shape[0]
    full = padded.shape[0]
    return pl.pallas_call(
        _bwd_conv_kernel,
        out_shape=(
            jax.ShapeDtypeStruct((rows, width), jnp.bfloat16),
            jax.ShapeDtypeStruct((taps, width), jnp.float32),
        ),
        grid=(width // LANES,),
        in_specs=[
            pl.BlockSpec((full, LANES), lambda c: (0, c)),
            pl.BlockSpec((rows, LANES), lambda c: (0, c)),
            pl.BlockSpec((full, LANES), lambda c: (0, c)),
            pl.BlockSpec((taps, LANES), lambda c: (0, c)),
        ],
        out_specs=(
            pl.BlockSpec((rows, LANES), lambda c: (0, c)),
            pl.BlockSpec((taps, LANES), lambda c: (0, c)),
        ),
    )(padded_grad, dmixed, padded, kernel)


def over_time(left, right):
    return lax.dot_general(
        left, right, (((0,), (0,)), ((), ())), preferred_element_type=jnp.float32
    )


def scatter_sum(parts, axis):
    got = lax.all_to_all(parts, axis, 0, 0, tiled=False)
    return jnp.sum(got, axis=0)


def gather_all(piece, axis):
    count = lax.axis_size(axis)
    spread = jnp.broadcast_to(piece[None], (count,) + piece.shape)
    return lax.all_to_all(spread, axis, 0, 0, tiled=False)


def split_rows(x, count):
    return x.reshape((count, x.shape[0] // count) + x.shape[1:])


def body(signal, readin, proj, kernel, gain, w_one, w_two, cotangent):
    rows = signal.shape[0]
    taps = kernel.shape[0]
    half = (taps - 1) // 2
    nn = lax.axis_size("neuron")
    nt = lax.axis_size("tm")
    me = lax.axis_index("neuron")
    share = rows // nn
    partial_latent = jnp.dot(signal, readin, preferred_element_type=jnp.float32)
    latent_rows = scatter_sum(split_rows(partial_latent, nn), "neuron").astype(jnp.bfloat16)
    latent = gather_all(latent_rows, "neuron").reshape(rows, -1)
    lifted = jnp.dot(latent, proj, preferred_element_type=jnp.float32)
    padded = with_halo(lifted, (("tm", 0),), half)
    mixed = fwd_conv(padded, lifted, kernel)
    scale = lax.rsqrt(jnp.mean(mixed * mixed, axis=1, keepdims=True) + 1e-05)
    normed = (mixed * scale * gain[None, :]).astype(jnp.bfloat16)
    pre = jnp.dot(normed, w_one, preferred_element_type=jnp.float32)
    act = jax.nn.silu(pre).astype(jnp.bfloat16)
    partial_mix = jnp.dot(act, w_two, preferred_element_type=jnp.float32)
    local_w_two = over_time(act, cotangent)
    dact = jnp.dot(cotangent, w_two.T, preferred_element_type=jnp.float32)
    sig = jax.nn.sigmoid(pre)
    dpre = (dact * sig * (1.0 + pre * (1.0 - sig))).astype(jnp.bfloat16)
    local_w_one = over_time(normed, dpre)
    partial_normed = jnp.dot(dpre, w_one.T, preferred_element_type=jnp.float32)
    dnormed_rows = scatter_sum(split_rows(partial_normed, nn), "neuron")
    dnormed = gather_all(dnormed_rows, "neuron").reshape(rows, -1)
    mix_rows = scatter_sum(split_rows(partial_mix, nn), "neuron")
    mixed_rows = lax.dynamic_slice_in_dim(mixed, me * share, share, 0)
    denoised_rows = (mixed_rows + mix_rows).astype(jnp.bfloat16)
    denoised = gather_all(denoised_rows, "neuron").reshape(rows, -1)
    local_gain = jnp.sum(dnormed * mixed * scale, axis=0)
    dgained = dnormed * gain[None, :]
    inner = jnp.mean(dgained * mixed, axis=1, keepdims=True)
    dmixed = cotangent.astype(jnp.float32) + scale * dgained - mixed * scale**3 * inner
    padded_grad = with_halo(dmixed, (("tm", 0),), half)
    dlifted, local_kernel = bwd_conv(padded_grad, dmixed, padded, kernel)
    local_proj = over_time(latent, dlifted)
    dlatent = jnp.dot(dlifted, proj.T, preferred_element_type=jnp.float32).astype(jnp.bfloat16)
    local_readin = over_time(signal, dlatent)
    grads = (local_proj, local_kernel, local_gain, local_w_one, local_w_two)
    width = local_readin.shape[1]
    small = jnp.concatenate([g.reshape(-1, width) for g in grads]).reshape(nt, -1, width)
    readin_part = local_readin.reshape(nt, -1, width)
    cut = readin_part.shape[1]
    packed = jnp.concatenate([readin_part, small], axis=1)
    denoised, packed = lax.optimization_barrier((denoised, packed))
    reduced = scatter_sum(packed, "tm")
    grad_readin = reduced[:cut]
    small_sum = gather_all(reduced[cut:], "tm").reshape(-1, width)
    outs = []
    at = 0
    for g in grads:
        count = g.size // width
        outs.append(small_sum[at:at + count].reshape(g.shape))
        at += count
    grad_proj, grad_kernel, grad_gain, grad_w_one, grad_w_two = outs
    return (denoised, grad_readin, grad_proj, grad_kernel, grad_gain, grad_w_one, grad_w_two)


def solution(mesh):
    in_specs = (
        P("tm", "neuron"),
        P("neuron", None),
        P(),
        P(),
        P(),
        P(None, "neuron"),
        P("neuron", None),
        P("tm", None),
    )
    out_specs = (
        P("tm", None),
        P(("neuron", "tm"), None),
        P(),
        P(),
        P(),
        P(None, "neuron"),
        P("neuron", None),
    )
    return jax.shard_map(body, mesh=mesh, in_specs=in_specs, out_specs=out_specs, check_vma=False)
```

```python
import jax
import jax.numpy as jnp
from jax import lax
from jax.experimental import pallas as pl
from jax.sharding import PartitionSpec as P

LANES = 128
CHUNK = 128
RCHUNK = 64


def with_halo(block, sides, width):
    for axis, dim in sides:
        count = lax.axis_size(axis)
        forward = [(i, i + 1) for i in range(count - 1)]
        backward = [(target, source) for source, target in forward]
        low = lax.ppermute(
            lax.slice_in_dim(block, block.shape[dim] - width, None, axis=dim), axis, forward
        )
        high = lax.ppermute(lax.slice_in_dim(block, 0, width, axis=dim), axis, backward)
        block = jnp.concatenate([low, block, high], axis=dim)
    return block


def _fwd_conv_kernel(x_ref, mid_ref, k_ref, o_ref):
    rows, lanes = o_ref.shape
    taps = k_ref.shape[0]
    for r0 in range(0, rows, CHUNK):
        acc = jnp.zeros((CHUNK, lanes), jnp.float32)
        for j in range(taps):
            acc = acc + k_ref[pl.ds(j, 1), :] * x_ref[pl.ds(r0 + j, CHUNK), :]
        o_ref[pl.ds(r0, CHUNK), :] = mid_ref[pl.ds(r0, CHUNK), :] + acc


def fwd_conv(padded, mid, kernel):
    rows, width = mid.shape
    taps = kernel.shape[0]
    return pl.pallas_call(
        _fwd_conv_kernel,
        out_shape=jax.ShapeDtypeStruct((rows, width), jnp.float32),
        grid=(width // LANES,),
        in_specs=[
            pl.BlockSpec((padded.shape[0], LANES), lambda c: (0, c)),
            pl.BlockSpec((rows, LANES), lambda c: (0, c)),
            pl.BlockSpec((taps, LANES), lambda c: (0, c)),
        ],
        out_specs=pl.BlockSpec((rows, LANES), lambda c: (0, c)),
    )(padded, mid, kernel)


def _bwd_conv_kernel(g_ref, d_ref, x_ref, k_ref, dl_ref, gk_ref):
    rows, lanes = dl_ref.shape
    taps = k_ref.shape[0]
    for r0 in range(0, rows, CHUNK):
        acc = jnp.zeros((CHUNK, lanes), jnp.float32)
        for j in range(taps):
            acc = acc + k_ref[pl.ds(taps - 1 - j, 1), :] * g_ref[pl.ds(r0 + j, CHUNK), :]
        dl_ref[pl.ds(r0, CHUNK), :] = (d_ref[pl.ds(r0, CHUNK), :] + acc).astype(dl_ref.dtype)
    for j in range(taps):
        part = jnp.zeros((8, lanes), jnp.float32)
        for r0 in range(0, rows, RCHUNK):
            prod = d_ref[pl.ds(r0, RCHUNK), :] * x_ref[pl.ds(r0 + j, RCHUNK), :]
            part = part + prod.reshape(RCHUNK // 8, 8, lanes).sum(axis=0)
        gk_ref[pl.ds(j, 1), :] = part.sum(axis=0, keepdims=True)


def bwd_conv(padded_grad, dmixed, padded, kernel):
    rows, width = dmixed.shape
    taps = kernel.shape[0]
    full = padded.shape[0]
    return pl.pallas_call(
        _bwd_conv_kernel,
        out_shape=(
            jax.ShapeDtypeStruct((rows, width), jnp.bfloat16),
            jax.ShapeDtypeStruct((taps, width), jnp.float32),
        ),
        grid=(width // LANES,),
        in_specs=[
            pl.BlockSpec((full, LANES), lambda c: (0, c)),
            pl.BlockSpec((rows, LANES), lambda c: (0, c)),
            pl.BlockSpec((full, LANES), lambda c: (0, c)),
            pl.BlockSpec((taps, LANES), lambda c: (0, c)),
        ],
        out_specs=(
            pl.BlockSpec((rows, LANES), lambda c: (0, c)),
            pl.BlockSpec((taps, LANES), lambda c: (0, c)),
        ),
    )(padded_grad, dmixed, padded, kernel)


def over_time(left, right):
    return lax.dot_general(
        left, right, (((0,), (0,)), ((), ())), preferred_element_type=jnp.float32
    )


def scatter_sum(parts, axis):
    got = lax.all_to_all(parts, axis, 0, 0, tiled=False)
    return jnp.sum(got, axis=0)


def gather_all(piece, axis):
    count = lax.axis_size(axis)
    spread = jnp.broadcast_to(piece[None], (count,) + piece.shape)
    return lax.all_to_all(spread, axis, 0, 0, tiled=False)


def split_rows(x, count):
    return x.reshape((count, x.shape[0] // count) + x.shape[1:])


def body(signal, readin, proj, kernel, gain, w_one, w_two, cotangent):
    rows = signal.shape[0]
    taps = kernel.shape[0]
    half = (taps - 1) // 2
    nn = lax.axis_size("neuron")
    nt = lax.axis_size("tm")
    me = lax.axis_index("neuron")
    share = rows // nn
    partial_latent = jnp.dot(signal, readin, preferred_element_type=jnp.float32)
    latent_rows = scatter_sum(split_rows(partial_latent, nn), "neuron").astype(jnp.bfloat16)
    latent = gather_all(latent_rows, "neuron").reshape(rows, -1)
    lifted = jnp.dot(latent, proj, preferred_element_type=jnp.float32)
    padded = with_halo(lifted, (("tm", 0),), half)
    mixed = fwd_conv(padded, lifted, kernel)
    scale = lax.rsqrt(jnp.mean(mixed * mixed, axis=1, keepdims=True) + 1e-05)
    normed = (mixed * scale * gain[None, :]).astype(jnp.bfloat16)
    pre = jnp.dot(normed, w_one, preferred_element_type=jnp.float32)
    act = jax.nn.silu(pre).astype(jnp.bfloat16)
    partial_mix = jnp.dot(act, w_two, preferred_element_type=jnp.float32)
    local_w_two = over_time(act, cotangent)
    dact = jnp.dot(cotangent, w_two.T, preferred_element_type=jnp.float32)
    sig = jax.nn.sigmoid(pre)
    dpre = (dact * sig * (1.0 + pre * (1.0 - sig))).astype(jnp.bfloat16)
    local_w_one = over_time(normed, dpre)
    partial_normed = jnp.dot(dpre, w_one.T, preferred_element_type=jnp.float32)
    dnormed_rows = scatter_sum(split_rows(partial_normed, nn), "neuron")
    dnormed = gather_all(dnormed_rows, "neuron").reshape(rows, -1)
    partial_mix, dnormed = lax.optimization_barrier((partial_mix, dnormed))
    mix_rows = scatter_sum(split_rows(partial_mix, nn), "neuron")
    mixed_rows = lax.dynamic_slice_in_dim(mixed, me * share, share, 0)
    denoised_rows = (mixed_rows + mix_rows).astype(jnp.bfloat16)
    denoised = gather_all(denoised_rows, "neuron").reshape(rows, -1)
    local_gain = jnp.sum(dnormed * mixed * scale, axis=0)
    dgained = dnormed * gain[None, :]
    inner = jnp.mean(dgained * mixed, axis=1, keepdims=True)
    dmixed = cotangent.astype(jnp.float32) + scale * dgained - mixed * scale**3 * inner
    padded_grad = with_halo(dmixed, (("tm", 0),), half)
    dlifted, local_kernel = bwd_conv(padded_grad, dmixed, padded, kernel)
    local_proj = over_time(latent, dlifted)
    dlatent = jnp.dot(dlifted, proj.T, preferred_element_type=jnp.float32).astype(jnp.bfloat16)
    local_readin = over_time(signal, dlatent)
    grads = (local_proj, local_kernel, local_gain, local_w_one, local_w_two)
    width = local_readin.shape[1]
    small = jnp.concatenate([g.reshape(-1, width) for g in grads]).reshape(nt, -1, width)
    readin_part = local_readin.reshape(nt, -1, width)
    cut = readin_part.shape[1]
    packed = jnp.concatenate([readin_part, small], axis=1)
    denoised, packed = lax.optimization_barrier((denoised, packed))
    reduced = scatter_sum(packed, "tm")
    grad_readin = reduced[:cut]
    small_sum = gather_all(reduced[cut:], "tm").reshape(-1, width)
    outs = []
    at = 0
    for g in grads:
        count = g.size // width
        outs.append(small_sum[at:at + count].reshape(g.shape))
        at += count
    grad_proj, grad_kernel, grad_gain, grad_w_one, grad_w_two = outs
    return (denoised, grad_readin, grad_proj, grad_kernel, grad_gain, grad_w_one, grad_w_two)


def solution(mesh):
    in_specs = (
        P("tm", "neuron"),
        P("neuron", None),
        P(),
        P(),
        P(),
        P(None, "neuron"),
        P("neuron", None),
        P("tm", None),
    )
    out_specs = (
        P("tm", None),
        P(("neuron", "tm"), None),
        P(),
        P(),
        P(),
        P(None, "neuron"),
        P("neuron", None),
    )
    return jax.shard_map(body, mesh=mesh, in_specs=in_specs, out_specs=out_specs, check_vma=False)
```

```python
import jax
import jax.numpy as jnp
from jax import lax
from jax.experimental import pallas as pl
from jax.sharding import PartitionSpec as P

LANES = 128
CHUNK = 128
RCHUNK = 64


def with_halo(block, sides, width):
    for axis, dim in sides:
        count = lax.axis_size(axis)
        forward = [(i, i + 1) for i in range(count - 1)]
        backward = [(target, source) for source, target in forward]
        low = lax.ppermute(
            lax.slice_in_dim(block, block.shape[dim] - width, None, axis=dim), axis, forward
        )
        high = lax.ppermute(lax.slice_in_dim(block, 0, width, axis=dim), axis, backward)
        block = jnp.concatenate([low, block, high], axis=dim)
    return block


def _fwd_conv_kernel(x_ref, mid_ref, k_ref, o_ref):
    rows, lanes = o_ref.shape
    taps = k_ref.shape[0]
    for r0 in range(0, rows, CHUNK):
        acc = jnp.zeros((CHUNK, lanes), jnp.float32)
        for j in range(taps):
            acc = acc + k_ref[pl.ds(j, 1), :] * x_ref[pl.ds(r0 + j, CHUNK), :]
        o_ref[pl.ds(r0, CHUNK), :] = mid_ref[pl.ds(r0, CHUNK), :] + acc


def fwd_conv(padded, mid, kernel):
    rows, width = mid.shape
    taps = kernel.shape[0]
    return pl.pallas_call(
        _fwd_conv_kernel,
        out_shape=jax.ShapeDtypeStruct((rows, width), jnp.float32),
        grid=(width // LANES,),
        in_specs=[
            pl.BlockSpec((padded.shape[0], LANES), lambda c: (0, c)),
            pl.BlockSpec((rows, LANES), lambda c: (0, c)),
            pl.BlockSpec((taps, LANES), lambda c: (0, c)),
        ],
        out_specs=pl.BlockSpec((rows, LANES), lambda c: (0, c)),
    )(padded, mid, kernel)


def _bwd_conv_kernel(g_ref, d_ref, x_ref, k_ref, dl_ref, gk_ref):
    rows, lanes = dl_ref.shape
    taps = k_ref.shape[0]
    for r0 in range(0, rows, CHUNK):
        acc = jnp.zeros((CHUNK, lanes), jnp.float32)
        for j in range(taps):
            acc = acc + k_ref[pl.ds(taps - 1 - j, 1), :] * g_ref[pl.ds(r0 + j, CHUNK), :]
        dl_ref[pl.ds(r0, CHUNK), :] = (d_ref[pl.ds(r0, CHUNK), :] + acc).astype(dl_ref.dtype)
    for j in range(taps):
        part = jnp.zeros((8, lanes), jnp.float32)
        for r0 in range(0, rows, RCHUNK):
            prod = d_ref[pl.ds(r0, RCHUNK), :] * x_ref[pl.ds(r0 + j, RCHUNK), :]
            part = part + prod.reshape(RCHUNK // 8, 8, lanes).sum(axis=0)
        gk_ref[pl.ds(j, 1), :] = part.sum(axis=0, keepdims=True)


def bwd_conv(padded_grad, dmixed, padded, kernel):
    rows, width = dmixed.shape
    taps = kernel.shape[0]
    full = padded.shape[0]
    return pl.pallas_call(
        _bwd_conv_kernel,
        out_shape=(
            jax.ShapeDtypeStruct((rows, width), jnp.bfloat16),
            jax.ShapeDtypeStruct((taps, width), jnp.float32),
        ),
        grid=(width // LANES,),
        in_specs=[
            pl.BlockSpec((full, LANES), lambda c: (0, c)),
            pl.BlockSpec((rows, LANES), lambda c: (0, c)),
            pl.BlockSpec((full, LANES), lambda c: (0, c)),
            pl.BlockSpec((taps, LANES), lambda c: (0, c)),
        ],
        out_specs=(
            pl.BlockSpec((rows, LANES), lambda c: (0, c)),
            pl.BlockSpec((taps, LANES), lambda c: (0, c)),
        ),
    )(padded_grad, dmixed, padded, kernel)


def over_time(left, right):
    return lax.dot_general(
        left, right, (((0,), (0,)), ((), ())), preferred_element_type=jnp.float32
    )


def scatter_sum(parts, axis):
    got = lax.all_to_all(parts, axis, 0, 0, tiled=False)
    return jnp.sum(got, axis=0)


def pair_scatter_sum(parts, axis):
    count, rows = parts.shape[0], parts.shape[1]
    core = lax.axis_index(axis) % 2
    pair = [(i, i ^ 1) for i in range(count)]
    grouped = parts.reshape((count // 2, 2) + parts.shape[1:])
    mine = lax.dynamic_index_in_dim(grouped, core, axis=1, keepdims=False)
    theirs = lax.dynamic_index_in_dim(grouped, 1 - core, axis=1, keepdims=False)
    chip = mine + lax.ppermute(theirs, axis, pair)
    first, second = chip[:, : rows // 2], chip[:, rows // 2 :]
    slabs = jnp.where(
        core == 0, jnp.stack([first, second], axis=1), jnp.stack([second, first], axis=1)
    ).reshape((count, rows // 2) + parts.shape[2:])
    got = lax.all_to_all(slabs, axis, 0, 0, tiled=False).reshape(
        (count // 2, 2, rows // 2) + parts.shape[2:]
    )
    same = jnp.sum(lax.dynamic_index_in_dim(got, core, axis=1, keepdims=False), axis=0)
    cross = jnp.sum(lax.dynamic_index_in_dim(got, 1 - core, axis=1, keepdims=False), axis=0)
    return jnp.concatenate([same, lax.ppermute(cross, axis, pair)], axis=0)


def gather_all(piece, axis):
    count = lax.axis_size(axis)
    spread = jnp.broadcast_to(piece[None], (count,) + piece.shape)
    return lax.all_to_all(spread, axis, 0, 0, tiled=False)


def split_rows(x, count):
    return x.reshape((count, x.shape[0] // count) + x.shape[1:])


def body(signal, readin, proj, kernel, gain, w_one, w_two, cotangent):
    rows = signal.shape[0]
    taps = kernel.shape[0]
    half = (taps - 1) // 2
    nn = lax.axis_size("neuron")
    nt = lax.axis_size("tm")
    me = lax.axis_index("neuron")
    share = rows // nn
    partial_latent = jnp.dot(signal, readin, preferred_element_type=jnp.float32)
    latent_rows = scatter_sum(split_rows(partial_latent, nn), "neuron").astype(jnp.bfloat16)
    latent = gather_all(latent_rows, "neuron").reshape(rows, -1)
    lifted = jnp.dot(latent, proj, preferred_element_type=jnp.float32)
    padded = with_halo(lifted, (("tm", 0),), half)
    mixed = fwd_conv(padded, lifted, kernel)
    scale = lax.rsqrt(jnp.mean(mixed * mixed, axis=1, keepdims=True) + 1e-05)
    normed = (mixed * scale * gain[None, :]).astype(jnp.bfloat16)
    pre = jnp.dot(normed, w_one, preferred_element_type=jnp.float32)
    act = jax.nn.silu(pre).astype(jnp.bfloat16)
    partial_mix = jnp.dot(act, w_two, preferred_element_type=jnp.float32)
    local_w_two = over_time(act, cotangent)
    dact = jnp.dot(cotangent, w_two.T, preferred_element_type=jnp.float32)
    sig = jax.nn.sigmoid(pre)
    dpre = (dact * sig * (1.0 + pre * (1.0 - sig))).astype(jnp.bfloat16)
    local_w_one = over_time(normed, dpre)
    partial_normed = jnp.dot(dpre, w_one.T, preferred_element_type=jnp.float32)
    dnormed_rows = scatter_sum(split_rows(partial_normed, nn), "neuron")
    dnormed = gather_all(dnormed_rows, "neuron").reshape(rows, -1)
    partial_mix, dnormed = lax.optimization_barrier((partial_mix, dnormed))
    mix_rows = scatter_sum(split_rows(partial_mix, nn), "neuron")
    mixed_rows = lax.dynamic_slice_in_dim(mixed, me * share, share, 0)
    denoised_rows = (mixed_rows + mix_rows).astype(jnp.bfloat16)
    denoised = gather_all(denoised_rows, "neuron").reshape(rows, -1)
    local_gain = jnp.sum(dnormed * mixed * scale, axis=0)
    dgained = dnormed * gain[None, :]
    inner = jnp.mean(dgained * mixed, axis=1, keepdims=True)
    dmixed = cotangent.astype(jnp.float32) + scale * dgained - mixed * scale**3 * inner
    padded_grad = with_halo(dmixed, (("tm", 0),), half)
    dlifted, local_kernel = bwd_conv(padded_grad, dmixed, padded, kernel)
    local_proj = over_time(latent, dlifted)
    dlatent = jnp.dot(dlifted, proj.T, preferred_element_type=jnp.float32).astype(jnp.bfloat16)
    local_readin = over_time(signal, dlatent)
    grads = (local_proj, local_kernel, local_gain, local_w_one, local_w_two)
    width = local_readin.shape[1]
    small = jnp.concatenate([g.reshape(-1, width) for g in grads]).reshape(nt, -1, width)
    readin_part = local_readin.reshape(nt, -1, width)
    cut = readin_part.shape[1]
    packed = jnp.concatenate([readin_part, small], axis=1)
    denoised, packed = lax.optimization_barrier((denoised, packed))
    reduced = pair_scatter_sum(packed, "tm")
    grad_readin = reduced[:cut]
    small_sum = gather_all(reduced[cut:], "tm").reshape(-1, width)
    outs = []
    at = 0
    for g in grads:
        count = g.size // width
        outs.append(small_sum[at:at + count].reshape(g.shape))
        at += count
    grad_proj, grad_kernel, grad_gain, grad_w_one, grad_w_two = outs
    return (denoised, grad_readin, grad_proj, grad_kernel, grad_gain, grad_w_one, grad_w_two)


def solution(mesh):
    in_specs = (
        P("tm", "neuron"),
        P("neuron", None),
        P(),
        P(),
        P(),
        P(None, "neuron"),
        P("neuron", None),
        P("tm", None),
    )
    out_specs = (
        P("tm", None),
        P(("neuron", "tm"), None),
        P(),
        P(),
        P(),
        P(None, "neuron"),
        P("neuron", None),
    )
    return jax.shard_map(body, mesh=mesh, in_specs=in_specs, out_specs=out_specs, check_vma=False)
```

```python
import jax
import jax.numpy as jnp
from jax import lax
from jax.experimental import pallas as pl
from jax.sharding import PartitionSpec as P

LANES = 128
CHUNK = 128
RCHUNK = 64


def with_halo(block, sides, width):
    for axis, dim in sides:
        count = lax.axis_size(axis)
        forward = [(i, i + 1) for i in range(count - 1)]
        backward = [(target, source) for source, target in forward]
        low = lax.ppermute(
            lax.slice_in_dim(block, block.shape[dim] - width, None, axis=dim), axis, forward
        )
        high = lax.ppermute(lax.slice_in_dim(block, 0, width, axis=dim), axis, backward)
        block = jnp.concatenate([low, block, high], axis=dim)
    return block


def _fwd_conv_kernel(x_ref, mid_ref, k_ref, o_ref):
    rows, lanes = o_ref.shape
    taps = k_ref.shape[0]
    for r0 in range(0, rows, CHUNK):
        acc = jnp.zeros((CHUNK, lanes), jnp.float32)
        for j in range(taps):
            acc = acc + k_ref[pl.ds(j, 1), :] * x_ref[pl.ds(r0 + j, CHUNK), :]
        o_ref[pl.ds(r0, CHUNK), :] = mid_ref[pl.ds(r0, CHUNK), :] + acc


def fwd_conv(padded, mid, kernel):
    rows, width = mid.shape
    taps = kernel.shape[0]
    return pl.pallas_call(
        _fwd_conv_kernel,
        out_shape=jax.ShapeDtypeStruct((rows, width), jnp.float32),
        grid=(width // LANES,),
        in_specs=[
            pl.BlockSpec((padded.shape[0], LANES), lambda c: (0, c)),
            pl.BlockSpec((rows, LANES), lambda c: (0, c)),
            pl.BlockSpec((taps, LANES), lambda c: (0, c)),
        ],
        out_specs=pl.BlockSpec((rows, LANES), lambda c: (0, c)),
    )(padded, mid, kernel)


def _bwd_conv_kernel(g_ref, d_ref, x_ref, k_ref, dl_ref, gk_ref):
    rows, lanes = dl_ref.shape
    taps = k_ref.shape[0]
    for r0 in range(0, rows, CHUNK):
        acc = jnp.zeros((CHUNK, lanes), jnp.float32)
        for j in range(taps):
            acc = acc + k_ref[pl.ds(taps - 1 - j, 1), :] * g_ref[pl.ds(r0 + j, CHUNK), :]
        dl_ref[pl.ds(r0, CHUNK), :] = (d_ref[pl.ds(r0, CHUNK), :] + acc).astype(dl_ref.dtype)
    for j in range(taps):
        part = jnp.zeros((8, lanes), jnp.float32)
        for r0 in range(0, rows, RCHUNK):
            prod = d_ref[pl.ds(r0, RCHUNK), :] * x_ref[pl.ds(r0 + j, RCHUNK), :]
            part = part + prod.reshape(RCHUNK // 8, 8, lanes).sum(axis=0)
        gk_ref[pl.ds(j, 1), :] = part.sum(axis=0, keepdims=True)


def bwd_conv(padded_grad, dmixed, padded, kernel):
    rows, width = dmixed.shape
    taps = kernel.shape[0]
    full = padded.shape[0]
    return pl.pallas_call(
        _bwd_conv_kernel,
        out_shape=(
            jax.ShapeDtypeStruct((rows, width), jnp.bfloat16),
            jax.ShapeDtypeStruct((taps, width), jnp.float32),
        ),
        grid=(width // LANES,),
        in_specs=[
            pl.BlockSpec((full, LANES), lambda c: (0, c)),
            pl.BlockSpec((rows, LANES), lambda c: (0, c)),
            pl.BlockSpec((full, LANES), lambda c: (0, c)),
            pl.BlockSpec((taps, LANES), lambda c: (0, c)),
        ],
        out_specs=(
            pl.BlockSpec((rows, LANES), lambda c: (0, c)),
            pl.BlockSpec((taps, LANES), lambda c: (0, c)),
        ),
    )(padded_grad, dmixed, padded, kernel)


def over_time(left, right):
    return lax.dot_general(
        left, right, (((0,), (0,)), ((), ())), preferred_element_type=jnp.float32
    )


def scatter_sum(parts, axis):
    got = lax.all_to_all(parts, axis, 0, 0, tiled=False)
    return jnp.sum(got, axis=0)


def pair_scatter_sum(parts, axis):
    count, rows = parts.shape[0], parts.shape[1]
    core = lax.axis_index(axis) % 2
    pair = [(i, i ^ 1) for i in range(count)]
    grouped = parts.reshape((count // 2, 2) + parts.shape[1:])
    mine = lax.dynamic_index_in_dim(grouped, core, axis=1, keepdims=False)
    theirs = lax.dynamic_index_in_dim(grouped, 1 - core, axis=1, keepdims=False)
    chip = mine + lax.ppermute(theirs, axis, pair)
    first, second = chip[:, : rows // 2], chip[:, rows // 2 :]
    slabs = jnp.where(
        core == 0, jnp.stack([first, second], axis=1), jnp.stack([second, first], axis=1)
    ).reshape((count, rows // 2) + parts.shape[2:])
    got = lax.all_to_all(slabs, axis, 0, 0, tiled=False).reshape(
        (count // 2, 2, rows // 2) + parts.shape[2:]
    )
    same = jnp.sum(lax.dynamic_index_in_dim(got, core, axis=1, keepdims=False), axis=0)
    cross = jnp.sum(lax.dynamic_index_in_dim(got, 1 - core, axis=1, keepdims=False), axis=0)
    return jnp.concatenate([same, lax.ppermute(cross, axis, pair)], axis=0)


def gather_all(piece, axis):
    count = lax.axis_size(axis)
    spread = jnp.broadcast_to(piece[None], (count,) + piece.shape)
    return lax.all_to_all(spread, axis, 0, 0, tiled=False)


def split_rows(x, count):
    return x.reshape((count, x.shape[0] // count) + x.shape[1:])


def body(signal, readin, proj, kernel, gain, w_one, w_two, cotangent):
    rows = signal.shape[0]
    taps = kernel.shape[0]
    half = (taps - 1) // 2
    nn = lax.axis_size("neuron")
    nt = lax.axis_size("tm")
    me = lax.axis_index("neuron")
    share = rows // nn
    partial_latent = jnp.dot(signal, readin, preferred_element_type=jnp.float32)
    latent_rows = scatter_sum(split_rows(partial_latent, nn), "neuron").astype(jnp.bfloat16)
    latent = gather_all(latent_rows, "neuron").reshape(rows, -1)
    lifted = jnp.dot(latent, proj, preferred_element_type=jnp.float32)
    padded = with_halo(lifted, (("tm", 0),), half)
    mixed = fwd_conv(padded, lifted, kernel)
    scale = lax.rsqrt(jnp.mean(mixed * mixed, axis=1, keepdims=True) + 1e-05)
    normed = (mixed * scale * gain[None, :]).astype(jnp.bfloat16)
    pre = jnp.dot(normed, w_one, preferred_element_type=jnp.float32)
    act = jax.nn.silu(pre).astype(jnp.bfloat16)
    partial_mix = jnp.dot(act, w_two, preferred_element_type=jnp.float32)
    local_w_two = over_time(act, cotangent)
    dact = jnp.dot(cotangent, w_two.T, preferred_element_type=jnp.float32)
    sig = jax.nn.sigmoid(pre)
    dpre = (dact * sig * (1.0 + pre * (1.0 - sig))).astype(jnp.bfloat16)
    local_w_one = over_time(normed, dpre)
    partial_normed = jnp.dot(dpre, w_one.T, preferred_element_type=jnp.float32)
    dnormed_rows = scatter_sum(split_rows(partial_normed, nn), "neuron")
    dnormed = gather_all(dnormed_rows, "neuron").reshape(rows, -1)
    local_gain = jnp.sum(dnormed * mixed * scale, axis=0)
    dgained = dnormed * gain[None, :]
    inner = jnp.mean(dgained * mixed, axis=1, keepdims=True)
    dmixed = cotangent.astype(jnp.float32) + scale * dgained - mixed * scale**3 * inner
    padded_grad = with_halo(dmixed, (("tm", 0),), half)
    dlifted, local_kernel = bwd_conv(padded_grad, dmixed, padded, kernel)
    partial_mix, dlifted = lax.optimization_barrier((partial_mix, dlifted))
    mix_rows = scatter_sum(split_rows(partial_mix, nn), "neuron")
    mixed_rows = lax.dynamic_slice_in_dim(mixed, me * share, share, 0)
    denoised_rows = (mixed_rows + mix_rows).astype(jnp.bfloat16)
    denoised = gather_all(denoised_rows, "neuron").reshape(rows, -1)
    local_proj = over_time(latent, dlifted)
    dlatent = jnp.dot(dlifted, proj.T, preferred_element_type=jnp.float32).astype(jnp.bfloat16)
    local_readin = over_time(signal, dlatent)
    grads = (local_proj, local_kernel, local_gain, local_w_one, local_w_two)
    width = local_readin.shape[1]
    small = jnp.concatenate([g.reshape(-1, width) for g in grads]).reshape(nt, -1, width)
    readin_part = local_readin.reshape(nt, -1, width)
    cut = readin_part.shape[1]
    packed = jnp.concatenate([readin_part, small], axis=1)
    reduced = pair_scatter_sum(packed, "tm")
    grad_readin = reduced[:cut]
    small_part = reduced[cut:]
    denoised, small_part = lax.optimization_barrier((denoised, small_part))
    small_sum = gather_all(small_part, "tm").reshape(-1, width)
    outs = []
    at = 0
    for g in grads:
        count = g.size // width
        outs.append(small_sum[at:at + count].reshape(g.shape))
        at += count
    grad_proj, grad_kernel, grad_gain, grad_w_one, grad_w_two = outs
    return (denoised, grad_readin, grad_proj, grad_kernel, grad_gain, grad_w_one, grad_w_two)


def solution(mesh):
    in_specs = (
        P("tm", "neuron"),
        P("neuron", None),
        P(),
        P(),
        P(),
        P(None, "neuron"),
        P("neuron", None),
        P("tm", None),
    )
    out_specs = (
        P("tm", None),
        P(("neuron", "tm"), None),
        P(),
        P(),
        P(),
        P(None, "neuron"),
        P("neuron", None),
    )
    return jax.shard_map(body, mesh=mesh, in_specs=in_specs, out_specs=out_specs, check_vma=False)
```

```python
import jax
import jax.numpy as jnp
from jax import lax
from jax.experimental import pallas as pl
from jax.sharding import PartitionSpec as P

LANES = 128
CHUNK = 128
RCHUNK = 64


def with_halo(block, sides, width):
    for axis, dim in sides:
        count = lax.axis_size(axis)
        forward = [(i, i + 1) for i in range(count - 1)]
        backward = [(target, source) for source, target in forward]
        low = lax.ppermute(
            lax.slice_in_dim(block, block.shape[dim] - width, None, axis=dim), axis, forward
        )
        high = lax.ppermute(lax.slice_in_dim(block, 0, width, axis=dim), axis, backward)
        block = jnp.concatenate([low, block, high], axis=dim)
    return block


def _fwd_conv_kernel(x_ref, mid_ref, k_ref, o_ref):
    rows, lanes = o_ref.shape
    taps = k_ref.shape[0]
    for r0 in range(0, rows, CHUNK):
        acc = jnp.zeros((CHUNK, lanes), jnp.float32)
        for j in range(taps):
            acc = acc + k_ref[pl.ds(j, 1), :] * x_ref[pl.ds(r0 + j, CHUNK), :]
        o_ref[pl.ds(r0, CHUNK), :] = mid_ref[pl.ds(r0, CHUNK), :] + acc


def fwd_conv(padded, mid, kernel):
    rows, width = mid.shape
    taps = kernel.shape[0]
    return pl.pallas_call(
        _fwd_conv_kernel,
        out_shape=jax.ShapeDtypeStruct((rows, width), jnp.float32),
        grid=(width // LANES,),
        in_specs=[
            pl.BlockSpec((padded.shape[0], LANES), lambda c: (0, c)),
            pl.BlockSpec((rows, LANES), lambda c: (0, c)),
            pl.BlockSpec((taps, LANES), lambda c: (0, c)),
        ],
        out_specs=pl.BlockSpec((rows, LANES), lambda c: (0, c)),
    )(padded, mid, kernel)


def _bwd_conv_kernel(g_ref, d_ref, x_ref, k_ref, dl_ref, gk_ref):
    rows, lanes = dl_ref.shape
    taps = k_ref.shape[0]
    for r0 in range(0, rows, CHUNK):
        acc = jnp.zeros((CHUNK, lanes), jnp.float32)
        for j in range(taps):
            acc = acc + k_ref[pl.ds(taps - 1 - j, 1), :] * g_ref[pl.ds(r0 + j, CHUNK), :]
        dl_ref[pl.ds(r0, CHUNK), :] = (d_ref[pl.ds(r0, CHUNK), :] + acc).astype(dl_ref.dtype)
    for j in range(taps):
        part = jnp.zeros((8, lanes), jnp.float32)
        for r0 in range(0, rows, RCHUNK):
            prod = d_ref[pl.ds(r0, RCHUNK), :] * x_ref[pl.ds(r0 + j, RCHUNK), :]
            part = part + prod.reshape(RCHUNK // 8, 8, lanes).sum(axis=0)
        gk_ref[pl.ds(j, 1), :] = part.sum(axis=0, keepdims=True)


def bwd_conv(padded_grad, dmixed, padded, kernel):
    rows, width = dmixed.shape
    taps = kernel.shape[0]
    full = padded.shape[0]
    return pl.pallas_call(
        _bwd_conv_kernel,
        out_shape=(
            jax.ShapeDtypeStruct((rows, width), jnp.bfloat16),
            jax.ShapeDtypeStruct((taps, width), jnp.float32),
        ),
        grid=(width // LANES,),
        in_specs=[
            pl.BlockSpec((full, LANES), lambda c: (0, c)),
            pl.BlockSpec((rows, LANES), lambda c: (0, c)),
            pl.BlockSpec((full, LANES), lambda c: (0, c)),
            pl.BlockSpec((taps, LANES), lambda c: (0, c)),
        ],
        out_specs=(
            pl.BlockSpec((rows, LANES), lambda c: (0, c)),
            pl.BlockSpec((taps, LANES), lambda c: (0, c)),
        ),
    )(padded_grad, dmixed, padded, kernel)


def over_time(left, right):
    return lax.dot_general(
        left, right, (((0,), (0,)), ((), ())), preferred_element_type=jnp.float32
    )


def scatter_sum(parts, axis):
    got = lax.all_to_all(parts, axis, 0, 0, tiled=False)
    return jnp.sum(got, axis=0)


def pair_scatter_sum(parts, axis):
    count, rows = parts.shape[0], parts.shape[1]
    core = lax.axis_index(axis) % 2
    pair = [(i, i ^ 1) for i in range(count)]
    grouped = parts.reshape((count // 2, 2) + parts.shape[1:])
    mine = lax.dynamic_index_in_dim(grouped, core, axis=1, keepdims=False)
    theirs = lax.dynamic_index_in_dim(grouped, 1 - core, axis=1, keepdims=False)
    chip = mine + lax.ppermute(theirs, axis, pair)
    first, second = chip[:, : rows // 2], chip[:, rows // 2 :]
    slabs = jnp.where(
        core == 0, jnp.stack([first, second], axis=1), jnp.stack([second, first], axis=1)
    ).reshape((count, rows // 2) + parts.shape[2:])
    got = lax.all_to_all(slabs, axis, 0, 0, tiled=False).reshape(
        (count // 2, 2, rows // 2) + parts.shape[2:]
    )
    same = jnp.sum(lax.dynamic_index_in_dim(got, core, axis=1, keepdims=False), axis=0)
    cross = jnp.sum(lax.dynamic_index_in_dim(got, 1 - core, axis=1, keepdims=False), axis=0)
    return jnp.concatenate([same, lax.ppermute(cross, axis, pair)], axis=0)


def gather_all(piece, axis):
    count = lax.axis_size(axis)
    spread = jnp.broadcast_to(piece[None], (count,) + piece.shape)
    return lax.all_to_all(spread, axis, 0, 0, tiled=False)


def split_rows(x, count):
    return x.reshape((count, x.shape[0] // count) + x.shape[1:])


def body(signal, readin, proj, kernel, gain, w_one, w_two, cotangent):
    rows = signal.shape[0]
    taps = kernel.shape[0]
    half = (taps - 1) // 2
    nn = lax.axis_size("neuron")
    nt = lax.axis_size("tm")
    me = lax.axis_index("neuron")
    share = rows // nn
    partial_latent = jnp.dot(signal, readin, preferred_element_type=jnp.float32)
    latent_rows = scatter_sum(split_rows(partial_latent, nn), "neuron").astype(jnp.bfloat16)
    latent = gather_all(latent_rows, "neuron").reshape(rows, -1)
    lifted = jnp.dot(latent, proj, preferred_element_type=jnp.float32)
    padded = with_halo(lifted, (("tm", 0),), half)
    mixed = fwd_conv(padded, lifted, kernel)
    scale = lax.rsqrt(jnp.mean(mixed * mixed, axis=1, keepdims=True) + 1e-05)
    normed = (mixed * scale * gain[None, :]).astype(jnp.bfloat16)
    pre = jnp.dot(normed, w_one, preferred_element_type=jnp.float32)
    act = jax.nn.silu(pre).astype(jnp.bfloat16)
    partial_mix = jnp.dot(act, w_two, preferred_element_type=jnp.float32)
    local_w_two = over_time(act, cotangent)
    dact = jnp.dot(cotangent, w_two.T, preferred_element_type=jnp.float32)
    sig = jax.nn.sigmoid(pre)
    dpre = (dact * sig * (1.0 + pre * (1.0 - sig))).astype(jnp.bfloat16)
    local_w_one = over_time(normed, dpre)
    partial_normed = jnp.dot(dpre, w_one.T, preferred_element_type=jnp.float32)
    dnormed_rows = scatter_sum(split_rows(partial_normed, nn), "neuron")
    dnormed = gather_all(dnormed_rows, "neuron").reshape(rows, -1)
    partial_mix, dnormed = lax.optimization_barrier((partial_mix, dnormed))
    mix_got = lax.all_to_all(split_rows(partial_mix, nn), "neuron", 0, 0, tiled=False)
    local_gain = jnp.sum(dnormed * mixed * scale, axis=0)
    dgained = dnormed * gain[None, :]
    inner = jnp.mean(dgained * mixed, axis=1, keepdims=True)
    dmixed = cotangent.astype(jnp.float32) + scale * dgained - mixed * scale**3 * inner
    padded_grad = with_halo(dmixed, (("tm", 0),), half)
    dlifted, local_kernel = bwd_conv(padded_grad, dmixed, padded, kernel)
    mix_got, dlifted = lax.optimization_barrier((mix_got, dlifted))
    mix_rows = jnp.sum(mix_got, axis=0)
    mixed_rows = lax.dynamic_slice_in_dim(mixed, me * share, share, 0)
    denoised_rows = (mixed_rows + mix_rows).astype(jnp.bfloat16)
    denoised = gather_all(denoised_rows, "neuron").reshape(rows, -1)
    local_proj = over_time(latent, dlifted)
    dlatent = jnp.dot(dlifted, proj.T, preferred_element_type=jnp.float32).astype(jnp.bfloat16)
    local_readin = over_time(signal, dlatent)
    grads = (local_proj, local_kernel, local_gain, local_w_one, local_w_two)
    width = local_readin.shape[1]
    small = jnp.concatenate([g.reshape(-1, width) for g in grads]).reshape(nt, -1, width)
    readin_part = local_readin.reshape(nt, -1, width)
    cut = readin_part.shape[1]
    packed = jnp.concatenate([readin_part, small], axis=1)
    denoised, packed = lax.optimization_barrier((denoised, packed))
    reduced = pair_scatter_sum(packed, "tm")
    grad_readin = reduced[:cut]
    small_sum = gather_all(reduced[cut:], "tm").reshape(-1, width)
    outs = []
    at = 0
    for g in grads:
        count = g.size // width
        outs.append(small_sum[at:at + count].reshape(g.shape))
        at += count
    grad_proj, grad_kernel, grad_gain, grad_w_one, grad_w_two = outs
    return (denoised, grad_readin, grad_proj, grad_kernel, grad_gain, grad_w_one, grad_w_two)


def solution(mesh):
    in_specs = (
        P("tm", "neuron"),
        P("neuron", None),
        P(),
        P(),
        P(),
        P(None, "neuron"),
        P("neuron", None),
        P("tm", None),
    )
    out_specs = (
        P("tm", None),
        P(("neuron", "tm"), None),
        P(),
        P(),
        P(),
        P(None, "neuron"),
        P("neuron", None),
    )
    return jax.shard_map(body, mesh=mesh, in_specs=in_specs, out_specs=out_specs, check_vma=False)
```

```python
import jax
import jax.numpy as jnp
from jax import lax
from jax.experimental import pallas as pl
from jax.sharding import PartitionSpec as P

LANES = 128
CHUNK = 128
RCHUNK = 64


def with_halo(block, sides, width):
    for axis, dim in sides:
        count = lax.axis_size(axis)
        forward = [(i, i + 1) for i in range(count - 1)]
        backward = [(target, source) for source, target in forward]
        low = lax.ppermute(
            lax.slice_in_dim(block, block.shape[dim] - width, None, axis=dim), axis, forward
        )
        high = lax.ppermute(lax.slice_in_dim(block, 0, width, axis=dim), axis, backward)
        block = jnp.concatenate([low, block, high], axis=dim)
    return block


def _fwd_conv_kernel(x_ref, mid_ref, k_ref, o_ref):
    rows, lanes = o_ref.shape
    taps = k_ref.shape[0]
    for r0 in range(0, rows, CHUNK):
        acc = jnp.zeros((CHUNK, lanes), jnp.float32)
        for j in range(taps):
            acc = acc + k_ref[pl.ds(j, 1), :] * x_ref[pl.ds(r0 + j, CHUNK), :]
        o_ref[pl.ds(r0, CHUNK), :] = mid_ref[pl.ds(r0, CHUNK), :] + acc


def fwd_conv(padded, mid, kernel):
    rows, width = mid.shape
    taps = kernel.shape[0]
    return pl.pallas_call(
        _fwd_conv_kernel,
        out_shape=jax.ShapeDtypeStruct((rows, width), jnp.float32),
        grid=(width // LANES,),
        in_specs=[
            pl.BlockSpec((padded.shape[0], LANES), lambda c: (0, c)),
            pl.BlockSpec((rows, LANES), lambda c: (0, c)),
            pl.BlockSpec((taps, LANES), lambda c: (0, c)),
        ],
        out_specs=pl.BlockSpec((rows, LANES), lambda c: (0, c)),
    )(padded, mid, kernel)


def _bwd_conv_kernel(g_ref, d_ref, x_ref, k_ref, dl_ref, gk_ref):
    rows, lanes = dl_ref.shape
    taps = k_ref.shape[0]
    for r0 in range(0, rows, CHUNK):
        acc = jnp.zeros((CHUNK, lanes), jnp.float32)
        for j in range(taps):
            acc = acc + k_ref[pl.ds(taps - 1 - j, 1), :] * g_ref[pl.ds(r0 + j, CHUNK), :]
        dl_ref[pl.ds(r0, CHUNK), :] = (d_ref[pl.ds(r0, CHUNK), :] + acc).astype(dl_ref.dtype)
    for j in range(taps):
        part = jnp.zeros((8, lanes), jnp.float32)
        for r0 in range(0, rows, RCHUNK):
            prod = d_ref[pl.ds(r0, RCHUNK), :] * x_ref[pl.ds(r0 + j, RCHUNK), :]
            part = part + prod.reshape(RCHUNK // 8, 8, lanes).sum(axis=0)
        gk_ref[pl.ds(j, 1), :] = part.sum(axis=0, keepdims=True)


def bwd_conv(padded_grad, dmixed, padded, kernel):
    rows, width = dmixed.shape
    taps = kernel.shape[0]
    full = padded.shape[0]
    return pl.pallas_call(
        _bwd_conv_kernel,
        out_shape=(
            jax.ShapeDtypeStruct((rows, width), jnp.bfloat16),
            jax.ShapeDtypeStruct((taps, width), jnp.float32),
        ),
        grid=(width // LANES,),
        in_specs=[
            pl.BlockSpec((full, LANES), lambda c: (0, c)),
            pl.BlockSpec((rows, LANES), lambda c: (0, c)),
            pl.BlockSpec((full, LANES), lambda c: (0, c)),
            pl.BlockSpec((taps, LANES), lambda c: (0, c)),
        ],
        out_specs=(
            pl.BlockSpec((rows, LANES), lambda c: (0, c)),
            pl.BlockSpec((taps, LANES), lambda c: (0, c)),
        ),
    )(padded_grad, dmixed, padded, kernel)


def over_time(left, right):
    return lax.dot_general(
        left, right, (((0,), (0,)), ((), ())), preferred_element_type=jnp.float32
    )


def scatter_sum(parts, axis):
    got = lax.all_to_all(parts, axis, 0, 0, tiled=False)
    return jnp.sum(got, axis=0)


def pair_scatter_sum(parts, axis):
    count, rows = parts.shape[0], parts.shape[1]
    core = lax.axis_index(axis) % 2
    pair = [(i, i ^ 1) for i in range(count)]
    grouped = parts.reshape((count // 2, 2) + parts.shape[1:])
    mine = lax.dynamic_index_in_dim(grouped, core, axis=1, keepdims=False)
    theirs = lax.dynamic_index_in_dim(grouped, 1 - core, axis=1, keepdims=False)
    chip = mine + lax.ppermute(theirs, axis, pair)
    first, second = chip[:, : rows // 2], chip[:, rows // 2 :]
    slabs = jnp.where(
        core == 0, jnp.stack([first, second], axis=1), jnp.stack([second, first], axis=1)
    ).reshape((count, rows // 2) + parts.shape[2:])
    got = lax.all_to_all(slabs, axis, 0, 0, tiled=False).reshape(
        (count // 2, 2, rows // 2) + parts.shape[2:]
    )
    same = jnp.sum(lax.dynamic_index_in_dim(got, core, axis=1, keepdims=False), axis=0)
    cross = jnp.sum(lax.dynamic_index_in_dim(got, 1 - core, axis=1, keepdims=False), axis=0)
    return jnp.concatenate([same, lax.ppermute(cross, axis, pair)], axis=0)


def gather_all(piece, axis):
    count = lax.axis_size(axis)
    spread = jnp.broadcast_to(piece[None], (count,) + piece.shape)
    return lax.all_to_all(spread, axis, 0, 0, tiled=False)


def split_rows(x, count):
    return x.reshape((count, x.shape[0] // count) + x.shape[1:])


def body(signal, readin, proj, kernel, gain, w_one, w_two, cotangent):
    rows = signal.shape[0]
    taps = kernel.shape[0]
    half = (taps - 1) // 2
    nn = lax.axis_size("neuron")
    nt = lax.axis_size("tm")
    me = lax.axis_index("neuron")
    share = rows // nn
    partial_latent = jnp.dot(signal, readin, preferred_element_type=jnp.float32)
    latent_rows = scatter_sum(split_rows(partial_latent, nn), "neuron").astype(jnp.bfloat16)
    latent = gather_all(latent_rows, "neuron").reshape(rows, -1)
    lifted = jnp.dot(latent, proj, preferred_element_type=jnp.float32)
    padded = with_halo(lifted, (("tm", 0),), half)
    mixed = fwd_conv(padded, lifted, kernel)
    scale = lax.rsqrt(jnp.mean(mixed * mixed, axis=1, keepdims=True) + 1e-05)
    normed = (mixed * scale * gain[None, :]).astype(jnp.bfloat16)
    pre = jnp.dot(normed, w_one, preferred_element_type=jnp.float32)
    act = jax.nn.silu(pre).astype(jnp.bfloat16)
    partial_mix = jnp.dot(act, w_two, preferred_element_type=jnp.float32)
    local_w_two = over_time(act, cotangent)
    dact = jnp.dot(cotangent, w_two.T, preferred_element_type=jnp.float32)
    sig = jax.nn.sigmoid(pre)
    dpre = (dact * sig * (1.0 + pre * (1.0 - sig))).astype(jnp.bfloat16)
    local_w_one = over_time(normed, dpre)
    partial_normed = jnp.dot(dpre, w_one.T, preferred_element_type=jnp.float32)
    dnormed_rows = scatter_sum(split_rows(partial_normed, nn), "neuron")
    dnormed = gather_all(dnormed_rows, "neuron").reshape(rows, -1)
    partial_mix, dnormed = lax.optimization_barrier((partial_mix, dnormed))
    mix_got = lax.all_to_all(split_rows(partial_mix, nn), "neuron", 0, 0, tiled=False)
    local_gain = jnp.sum(dnormed * mixed * scale, axis=0)
    dgained = dnormed * gain[None, :]
    inner = jnp.mean(dgained * mixed, axis=1, keepdims=True)
    dmixed = cotangent.astype(jnp.float32) + scale * dgained - mixed * scale**3 * inner
    padded_grad = with_halo(dmixed, (("tm", 0),), half)
    dlifted, local_kernel = bwd_conv(padded_grad, dmixed, padded, kernel)
    local_proj = over_time(latent, dlifted)
    dlatent = jnp.dot(dlifted, proj.T, preferred_element_type=jnp.float32).astype(jnp.bfloat16)
    local_readin = over_time(signal, dlatent)
    mix_got, local_readin = lax.optimization_barrier((mix_got, local_readin))
    mix_rows = jnp.sum(mix_got, axis=0)
    mixed_rows = lax.dynamic_slice_in_dim(mixed, me * share, share, 0)
    denoised_rows = (mixed_rows + mix_rows).astype(jnp.bfloat16)
    denoised = gather_all(denoised_rows, "neuron").reshape(rows, -1)
    grads = (local_proj, local_kernel, local_gain, local_w_one, local_w_two)
    width = local_readin.shape[1]
    small = jnp.concatenate([g.reshape(-1, width) for g in grads]).reshape(nt, -1, width)
    readin_part = local_readin.reshape(nt, -1, width)
    cut = readin_part.shape[1]
    packed = jnp.concatenate([readin_part, small], axis=1)
    denoised, packed = lax.optimization_barrier((denoised, packed))
    reduced = pair_scatter_sum(packed, "tm")
    grad_readin = reduced[:cut]
    small_sum = gather_all(reduced[cut:], "tm").reshape(-1, width)
    outs = []
    at = 0
    for g in grads:
        count = g.size // width
        outs.append(small_sum[at:at + count].reshape(g.shape))
        at += count
    grad_proj, grad_kernel, grad_gain, grad_w_one, grad_w_two = outs
    return (denoised, grad_readin, grad_proj, grad_kernel, grad_gain, grad_w_one, grad_w_two)


def solution(mesh):
    in_specs = (
        P("tm", "neuron"),
        P("neuron", None),
        P(),
        P(),
        P(),
        P(None, "neuron"),
        P("neuron", None),
        P("tm", None),
    )
    out_specs = (
        P("tm", None),
        P(("neuron", "tm"), None),
        P(),
        P(),
        P(),
        P(None, "neuron"),
        P("neuron", None),
    )
    return jax.shard_map(body, mesh=mesh, in_specs=in_specs, out_specs=out_specs, check_vma=False)
```

```python
import jax
import jax.numpy as jnp
from jax import lax
from jax.experimental import pallas as pl
from jax.sharding import PartitionSpec as P

LANES = 128
CHUNK = 128
RCHUNK = 64


def with_halo(block, sides, width):
    for axis, dim in sides:
        count = lax.axis_size(axis)
        forward = [(i, i + 1) for i in range(count - 1)]
        backward = [(target, source) for source, target in forward]
        low = lax.ppermute(
            lax.slice_in_dim(block, block.shape[dim] - width, None, axis=dim), axis, forward
        )
        high = lax.ppermute(lax.slice_in_dim(block, 0, width, axis=dim), axis, backward)
        block = jnp.concatenate([low, block, high], axis=dim)
    return block


def _fwd_conv_kernel(x_ref, mid_ref, k_ref, o_ref):
    rows, lanes = o_ref.shape
    taps = k_ref.shape[0]
    for r0 in range(0, rows, CHUNK):
        acc = jnp.zeros((CHUNK, lanes), jnp.float32)
        for j in range(taps):
            acc = acc + k_ref[pl.ds(j, 1), :] * x_ref[pl.ds(r0 + j, CHUNK), :]
        o_ref[pl.ds(r0, CHUNK), :] = mid_ref[pl.ds(r0, CHUNK), :] + acc


def fwd_conv(padded, mid, kernel):
    rows, width = mid.shape
    taps = kernel.shape[0]
    return pl.pallas_call(
        _fwd_conv_kernel,
        out_shape=jax.ShapeDtypeStruct((rows, width), jnp.float32),
        grid=(width // LANES,),
        in_specs=[
            pl.BlockSpec((padded.shape[0], LANES), lambda c: (0, c)),
            pl.BlockSpec((rows, LANES), lambda c: (0, c)),
            pl.BlockSpec((taps, LANES), lambda c: (0, c)),
        ],
        out_specs=pl.BlockSpec((rows, LANES), lambda c: (0, c)),
    )(padded, mid, kernel)


def _bwd_conv_kernel(g_ref, d_ref, x_ref, k_ref, dl_ref, gk_ref):
    rows, lanes = dl_ref.shape
    taps = k_ref.shape[0]
    for r0 in range(0, rows, CHUNK):
        acc = jnp.zeros((CHUNK, lanes), jnp.float32)
        for j in range(taps):
            acc = acc + k_ref[pl.ds(taps - 1 - j, 1), :] * g_ref[pl.ds(r0 + j, CHUNK), :]
        dl_ref[pl.ds(r0, CHUNK), :] = (d_ref[pl.ds(r0, CHUNK), :] + acc).astype(dl_ref.dtype)
    for j in range(taps):
        part = jnp.zeros((8, lanes), jnp.float32)
        for r0 in range(0, rows, RCHUNK):
            prod = d_ref[pl.ds(r0, RCHUNK), :] * x_ref[pl.ds(r0 + j, RCHUNK), :]
            part = part + prod.reshape(RCHUNK // 8, 8, lanes).sum(axis=0)
        gk_ref[pl.ds(j, 1), :] = part.sum(axis=0, keepdims=True)


def bwd_conv(padded_grad, dmixed, padded, kernel):
    rows, width = dmixed.shape
    taps = kernel.shape[0]
    full = padded.shape[0]
    return pl.pallas_call(
        _bwd_conv_kernel,
        out_shape=(
            jax.ShapeDtypeStruct((rows, width), jnp.bfloat16),
            jax.ShapeDtypeStruct((taps, width), jnp.float32),
        ),
        grid=(width // LANES,),
        in_specs=[
            pl.BlockSpec((full, LANES), lambda c: (0, c)),
            pl.BlockSpec((rows, LANES), lambda c: (0, c)),
            pl.BlockSpec((full, LANES), lambda c: (0, c)),
            pl.BlockSpec((taps, LANES), lambda c: (0, c)),
        ],
        out_specs=(
            pl.BlockSpec((rows, LANES), lambda c: (0, c)),
            pl.BlockSpec((taps, LANES), lambda c: (0, c)),
        ),
    )(padded_grad, dmixed, padded, kernel)


def over_time(left, right):
    return lax.dot_general(
        left, right, (((0,), (0,)), ((), ())), preferred_element_type=jnp.float32
    )


def scatter_sum(parts, axis):
    got = lax.all_to_all(parts, axis, 0, 0, tiled=False)
    return jnp.sum(got, axis=0)


def pair_scatter_sum(parts, axis):
    count, rows = parts.shape[0], parts.shape[1]
    core = lax.axis_index(axis) % 2
    pair = [(i, i ^ 1) for i in range(count)]
    grouped = parts.reshape((count // 2, 2) + parts.shape[1:])
    mine = lax.dynamic_index_in_dim(grouped, core, axis=1, keepdims=False)
    theirs = lax.dynamic_index_in_dim(grouped, 1 - core, axis=1, keepdims=False)
    chip = mine + lax.ppermute(theirs, axis, pair)
    first, second = chip[:, : rows // 2], chip[:, rows // 2 :]
    slabs = jnp.where(
        core == 0, jnp.stack([first, second], axis=1), jnp.stack([second, first], axis=1)
    ).reshape((count, rows // 2) + parts.shape[2:])
    got = lax.all_to_all(slabs, axis, 0, 0, tiled=False).reshape(
        (count // 2, 2, rows // 2) + parts.shape[2:]
    )
    same = jnp.sum(lax.dynamic_index_in_dim(got, core, axis=1, keepdims=False), axis=0)
    cross = jnp.sum(lax.dynamic_index_in_dim(got, 1 - core, axis=1, keepdims=False), axis=0)
    return jnp.concatenate([same, lax.ppermute(cross, axis, pair)], axis=0)


def gather_all(piece, axis):
    count = lax.axis_size(axis)
    spread = jnp.broadcast_to(piece[None], (count,) + piece.shape)
    return lax.all_to_all(spread, axis, 0, 0, tiled=False)


def split_rows(x, count):
    return x.reshape((count, x.shape[0] // count) + x.shape[1:])


def body(signal, readin, proj, kernel, gain, w_one, w_two, cotangent):
    rows = signal.shape[0]
    taps = kernel.shape[0]
    half = (taps - 1) // 2
    nn = lax.axis_size("neuron")
    nt = lax.axis_size("tm")
    me = lax.axis_index("neuron")
    share = rows // nn
    partial_latent = jnp.dot(signal, readin, preferred_element_type=jnp.float32)
    latent_rows = scatter_sum(split_rows(partial_latent, nn), "neuron").astype(jnp.bfloat16)
    latent = gather_all(latent_rows, "neuron").reshape(rows, -1)
    lifted = jnp.dot(latent, proj, preferred_element_type=jnp.float32)
    padded = with_halo(lifted, (("tm", 0),), half)
    mixed = fwd_conv(padded, lifted, kernel)
    scale = lax.rsqrt(jnp.mean(mixed * mixed, axis=1, keepdims=True) + 1e-05)
    normed = (mixed * scale * gain[None, :]).astype(jnp.bfloat16)
    pre = jnp.dot(normed, w_one, preferred_element_type=jnp.float32)
    act = jax.nn.silu(pre).astype(jnp.bfloat16)
    partial_mix = jnp.dot(act, w_two, preferred_element_type=jnp.float32)
    local_w_two = over_time(act, cotangent)
    dact = jnp.dot(cotangent, w_two.T, preferred_element_type=jnp.float32)
    sig = jax.nn.sigmoid(pre)
    dpre = (dact * sig * (1.0 + pre * (1.0 - sig))).astype(jnp.bfloat16)
    local_w_one = over_time(normed, dpre)
    partial_normed = jnp.dot(dpre, w_one.T, preferred_element_type=jnp.float32)
    dnormed_rows = scatter_sum(split_rows(partial_normed, nn), "neuron")
    own = lambda x: lax.dynamic_slice_in_dim(x, me * share, share, 0)
    mixed_own, scale_own = own(mixed), own(scale)
    gain_part = jnp.sum(dnormed_rows * mixed_own * scale_own, axis=0)
    dgained = dnormed_rows * gain[None, :]
    inner = jnp.mean(dgained * mixed_own, axis=1, keepdims=True)
    dmixed_own = (
        own(cotangent).astype(jnp.float32)
        + scale_own * dgained
        - mixed_own * scale_own**3 * inner
    )
    got = gather_all(jnp.concatenate([dmixed_own, gain_part[None, :]], axis=0), "neuron")
    dmixed = got[:, :share].reshape(rows, -1)
    local_gain = jnp.sum(got[:, share], axis=0)
    partial_mix, dmixed = lax.optimization_barrier((partial_mix, dmixed))
    mix_got = lax.all_to_all(split_rows(partial_mix, nn), "neuron", 0, 0, tiled=False)
    padded_grad = with_halo(dmixed, (("tm", 0),), half)
    dlifted, local_kernel = bwd_conv(padded_grad, dmixed, padded, kernel)
    mix_got, dlifted = lax.optimization_barrier((mix_got, dlifted))
    mix_rows = jnp.sum(mix_got, axis=0)
    mixed_rows = lax.dynamic_slice_in_dim(mixed, me * share, share, 0)
    denoised_rows = (mixed_rows + mix_rows).astype(jnp.bfloat16)
    denoised = gather_all(denoised_rows, "neuron").reshape(rows, -1)
    local_proj = over_time(latent, dlifted)
    dlatent = jnp.dot(dlifted, proj.T, preferred_element_type=jnp.float32).astype(jnp.bfloat16)
    local_readin = over_time(signal, dlatent)
    grads = (local_proj, local_kernel, local_gain, local_w_one, local_w_two)
    width = local_readin.shape[1]
    small = jnp.concatenate([g.reshape(-1, width) for g in grads]).reshape(nt, -1, width)
    readin_part = local_readin.reshape(nt, -1, width)
    cut = readin_part.shape[1]
    packed = jnp.concatenate([readin_part, small], axis=1)
    denoised, packed = lax.optimization_barrier((denoised, packed))
    reduced = pair_scatter_sum(packed, "tm")
    grad_readin = reduced[:cut]
    small_sum = gather_all(reduced[cut:], "tm").reshape(-1, width)
    outs = []
    at = 0
    for g in grads:
        count = g.size // width
        outs.append(small_sum[at:at + count].reshape(g.shape))
        at += count
    grad_proj, grad_kernel, grad_gain, grad_w_one, grad_w_two = outs
    return (denoised, grad_readin, grad_proj, grad_kernel, grad_gain, grad_w_one, grad_w_two)


def solution(mesh):
    in_specs = (
        P("tm", "neuron"),
        P("neuron", None),
        P(),
        P(),
        P(),
        P(None, "neuron"),
        P("neuron", None),
        P("tm", None),
    )
    out_specs = (
        P("tm", None),
        P(("neuron", "tm"), None),
        P(),
        P(),
        P(),
        P(None, "neuron"),
        P("neuron", None),
    )
    return jax.shard_map(body, mesh=mesh, in_specs=in_specs, out_specs=out_specs, check_vma=False)
```
